256 devices in a mesh: ch: 64 (over z_lo, y, x), ta: 4 (over z_hi, core).
Axes of the slice: x: 4, y: 4, z: 8 (z_hi: 2, z_lo: 4; z = z_hi * 4 + z_lo), core: 2. Of those that a mesh axis runs over, the one named last changes fastest.
Arguments:
- raw: bfloat16 [16384, 20480], P('ch', 'ta'), may hold values from -40 to 40
- fir_taps: bfloat16 [129], replicated, may hold values from -0.5 to 0.5
- start_basis: float32 [512, 16], replicated, may hold values from -6 to 6
Outputs:
- cleaned: bfloat16 [16384, 20480], P('ch', 'ta')
The draws below stay inside these ranges and needn't reach their ends.
All inputs are finite; a program needn't handle non-finite values.
Results may differ from the reference program's by a relative error of at most 0.008.
Values may be sent and summed in bfloat16 or wider, within the bound.
No kernel may reach another device: no remote copies, remote signals or barrier semaphores. Data moves between devices by JAX's collectives and lax.ppermute only.
A program may use at most 64 MiB of HBM per device.

```python
import math
import jax
import jax.numpy as jnp
from jax import lax

TAPS = 129
GAUGE = 4
STRIDE = 128
RANK = 16
ITERS = 6
WIN = 512
CHANNELS = 16384
TIME = 20480


def draw_raw(key, part):
    keys = jax.random.split(key, 4)
    noise = jnp.clip(jax.random.normal(keys[0], (CHANNELS, TIME), jnp.float32), -5.0, 5.0)
    scales = jnp.exp(jax.random.uniform(keys[1], (CHANNELS, 1), jnp.float32, jnp.log(0.3), jnp.log(3.0)))
    common = jnp.clip(jax.random.normal(keys[2], (1, TIME), jnp.float32), -4.0, 4.0)
    couple = 1.5 * jnp.clip(jax.random.normal(keys[3], (CHANNELS, 1), jnp.float32), -4.0, 4.0)
    values = scales * noise + couple * common
    return values.astype(jnp.bfloat16)


def scatter_about(stream_key, shape, scale, most, kind=jnp.bfloat16):
    result = jax.random.normal(stream_key, shape, jnp.float32) * scale
    return jnp.minimum(jnp.maximum(result, -most), most).astype(kind)


def setup_inputs(seed: int = 0) -> dict:
    key_list = jax.random.split(jax.random.key(seed), 4)
    raw = draw_raw(jax.random.fold_in(key_list[3], 71), 0)
    fir_taps = scatter_about(key_list[1], (TAPS,), TAPS ** -0.5, 0.5)
    start_basis = scatter_about(key_list[2], (WIN, RANK), 1.0, 6.0, jnp.float32)
    return {"raw": raw, "fir_taps": fir_taps, "start_basis": start_basis}


def toeplitz_band(taps, width):
    count = taps.shape[0]
    line = jnp.concatenate([taps, jnp.zeros((width,), taps.dtype)])
    flat = jnp.tile(line, width)[:width * (count + width - 1)]
    return flat.reshape(width, count + width - 1).T

def orthonormal(image):
    gram = jnp.dot(image.T, image, precision=lax.Precision.HIGHEST)
    lower = jnp.linalg.cholesky(gram)
    return lax.linalg.triangular_solve(lower, image, left_side=False, lower=True, transpose_a=True)

def reference(raw, fir_taps, start_basis):
    half = (TAPS - 1) // 2
    width = math.gcd(TIME, 512)
    padded = jnp.pad(raw, ((0, 0), (half, half)))
    band_matrix = toeplitz_band(fir_taps, width)

    def fir_block(number):
        piece = lax.dynamic_slice_in_dim(padded, number * width, width + TAPS - 1, 1)
        return jnp.dot(piece.astype(jnp.float32), band_matrix.astype(jnp.float32), preferred_element_type=jnp.float32)
    blocks = lax.map(fir_block, jnp.arange(TIME // width, dtype=jnp.int32))
    filtered = jnp.transpose(blocks, (1, 0, 2)).reshape(CHANNELS, TIME)
    rimmed = jnp.pad(filtered, ((GAUGE, GAUGE), (0, 0)))
    gauged = (rimmed[2 * GAUGE:] - rimmed[:-2 * GAUGE]).astype(jnp.bfloat16)
    framed = jnp.pad(gauged, ((2 * STRIDE, STRIDE), (0, 0)))

    def window(number):
        frame = lax.dynamic_slice_in_dim(framed, number * STRIDE, WIN, 0)
        scatter_mat = jnp.dot(frame.astype(jnp.float32), frame.T.astype(jnp.float32), preferred_element_type=jnp.float32) / TIME
        basis = start_basis
        for sweep in range(ITERS):
            basis = orthonormal(jnp.dot(scatter_mat, basis, precision=lax.Precision.HIGHEST))
        rounded = basis.astype(jnp.bfloat16)
        coeffs = jnp.dot(rounded.T.astype(jnp.float32), frame.astype(jnp.float32), preferred_element_type=jnp.float32).astype(jnp.bfloat16)
        fitted = jnp.dot(rounded[2 * STRIDE:3 * STRIDE].astype(jnp.float32), coeffs.astype(jnp.float32), preferred_element_type=jnp.float32)
        return (frame[2 * STRIDE:3 * STRIDE].astype(jnp.float32) - fitted).astype(jnp.bfloat16)
    cleaned = lax.map(window, jnp.arange(CHANNELS // STRIDE, dtype=jnp.int32))
    return cleaned.reshape(CHANNELS, TIME)
```

```python
import math

import jax
import jax.numpy as jnp
from jax import lax
from jax.experimental import pallas as pl
from jax.experimental.pallas import tpu as pltpu
from jax.sharding import PartitionSpec as P

TAPS = 129
GAUGE = 4
STRIDE = 128
RANK = 16
ITERS = 6
WIN = 512


def with_halo(block, sides, width):
    for axis, dim in sides:
        count = lax.axis_size(axis)
        forward = [(i, i + 1) for i in range(count - 1)]
        backward = [(target, source) for source, target in forward]
        low = lax.ppermute(
            lax.slice_in_dim(block, block.shape[dim] - width, None, axis=dim), axis, forward
        )
        high = lax.ppermute(lax.slice_in_dim(block, 0, width, axis=dim), axis, backward)
        block = jnp.concatenate([low, block, high], axis=dim)
    return block


def shifted(value, axis, steps):
    count = lax.axis_size(axis)
    first, last = (max(0, -steps), min(count, count - steps))
    return lax.ppermute(value, axis, [(source, source + steps) for source in range(first, last)])


def toeplitz_band(taps, width):
    count = taps.shape[0]
    line = jnp.concatenate([taps, jnp.zeros((width,), taps.dtype)])
    flat = jnp.tile(line, width)[: width * (count + width - 1)]
    return flat.reshape(width, count + width - 1).T


def gram(a, b):
    return lax.dot_general(a, b, (((1,), (1,)), ((), ())), preferred_element_type=jnp.float32)


def orthonormal_rows(image, rows):
    result = image
    for i in range(image.shape[0]):
        row = result[i : i + 1, :]
        unit = row / jnp.sqrt(jnp.sum(row * row, axis=1, keepdims=True))
        proj = jnp.sum(result * unit, axis=1, keepdims=True)
        result = jnp.where(rows > i, result - proj * unit, jnp.where(rows == i, unit, result))
    return result


def subspace_kernel(band_ref, start_ref, out_ref):
    windows = out_ref.shape[0]
    rank, win = start_ref.shape
    rows = lax.broadcasted_iota(jnp.int32, (rank, 1), 0)
    bases = [start_ref[...] for _ in range(windows)]
    for sweep in range(ITERS):
        for number in range(windows):
            lo = number * STRIDE
            scatter_mat = band_ref[lo : lo + win, lo : lo + win]
            image = jnp.dot(
                bases[number], scatter_mat, precision=lax.Precision.HIGHEST,
                preferred_element_type=jnp.float32,
            )
            bases[number] = orthonormal_rows(image, rows)
    for number in range(windows):
        out_ref[number] = bases[number].astype(out_ref.dtype)


def subspace(band, start_t, windows):
    return pl.pallas_call(
        subspace_kernel,
        out_shape=jax.ShapeDtypeStruct((windows,) + start_t.shape, jnp.bfloat16),
        in_specs=[
            pl.BlockSpec(memory_space=pltpu.VMEM),
            pl.BlockSpec(memory_space=pltpu.VMEM),
        ],
        out_specs=pl.BlockSpec(memory_space=pltpu.VMEM),
    )(band, start_t)


def per_device(raw, fir_taps, start_basis):
    chans = raw.shape[0]
    samples = raw.shape[1]
    half = (TAPS - 1) // 2
    width = math.gcd(samples, 256)
    padded = with_halo(raw, (("ta", 1),), half)
    band_matrix = toeplitz_band(fir_taps, width)
    pieces = jnp.stack(
        [
            padded[:, number * width : number * width + width + TAPS - 1]
            for number in range(samples // width)
        ]
    )
    filtered = jnp.einsum(
        "bct,tu->cbu", pieces, band_matrix, preferred_element_type=jnp.float32
    ).reshape(chans, samples)
    extended = with_halo(filtered, (("ch", 0),), GAUGE)
    gauged = (extended[2 * GAUGE :] - extended[: -2 * GAUGE]).astype(jnp.bfloat16)

    tiles = chans // STRIDE
    windows = tiles
    total_time = samples * lax.axis_size("ta")
    lower_part = shifted(gauged[chans - 2 * STRIDE :], "ch", 1)
    upper_part = shifted(gauged[:STRIDE], "ch", -1)

    own = lax.psum(gram(gauged, gauged), "ta")
    own_left = shifted(own[chans - 2 * STRIDE :, chans - 2 * STRIDE :], "ch", 1)
    own_right = shifted(own[:STRIDE, :STRIDE], "ch", -1)

    own, lower_part, upper_part = lax.optimization_barrier((own, lower_part, upper_part))
    cross_left = gram(lower_part, gauged)
    tail = jnp.concatenate([lower_part[STRIDE:], gauged], axis=0)
    cross_right = gram(tail, upper_part)
    cross_left, cross_right = lax.psum((cross_left, cross_right), "ta")

    zeros = jnp.zeros((STRIDE, STRIDE), jnp.float32)
    top = jnp.concatenate(
        [own_left, cross_left, jnp.concatenate([zeros, cross_right[:STRIDE]], axis=0)], axis=1
    )
    middle = jnp.concatenate(
        [cross_left.T, own, cross_right[STRIDE:]], axis=1
    )
    corner = jnp.concatenate([zeros, cross_right[:STRIDE].T], axis=1)
    bottom = jnp.concatenate([corner, cross_right[STRIDE:].T, own_right], axis=1)
    band = jnp.concatenate([top, middle, bottom], axis=0) / total_time

    rounded = subspace(band, start_basis.T, windows)

    stacked = jnp.concatenate([lower_part, gauged, upper_part], axis=0)
    outputs = []
    for number in range(windows):
        frame = stacked[number * STRIDE : number * STRIDE + WIN]
        coeffs = jnp.dot(rounded[number], frame, preferred_element_type=jnp.float32).astype(
            jnp.bfloat16
        )
        fitted = lax.dot_general(
            rounded[number, :, 2 * STRIDE : 3 * STRIDE], coeffs, (((0,), (0,)), ((), ())),
            preferred_element_type=jnp.float32,
        )
        outputs.append(
            (frame[2 * STRIDE : 3 * STRIDE].astype(jnp.float32) - fitted).astype(jnp.bfloat16)
        )
    return jnp.concatenate(outputs, axis=0)


def solution(mesh):
    return jax.shard_map(
        per_device,
        mesh=mesh,
        in_specs=(P("ch", "ta"), P(), P()),
        out_specs=P("ch", "ta"),
        check_vma=False,
    )
```

```python
import math

import jax
import jax.numpy as jnp
from jax import lax
from jax.experimental import pallas as pl
from jax.experimental.pallas import tpu as pltpu
from jax.sharding import PartitionSpec as P

TAPS = 129
GAUGE = 4
STRIDE = 128
RANK = 16
ITERS = 6
WIN = 512


def with_halo(block, sides, width):
    for axis, dim in sides:
        count = lax.axis_size(axis)
        forward = [(i, i + 1) for i in range(count - 1)]
        backward = [(target, source) for source, target in forward]
        low = lax.ppermute(
            lax.slice_in_dim(block, block.shape[dim] - width, None, axis=dim), axis, forward
        )
        high = lax.ppermute(lax.slice_in_dim(block, 0, width, axis=dim), axis, backward)
        block = jnp.concatenate([low, block, high], axis=dim)
    return block


def shifted(value, axis, steps):
    count = lax.axis_size(axis)
    first, last = (max(0, -steps), min(count, count - steps))
    return lax.ppermute(value, axis, [(source, source + steps) for source in range(first, last)])


def toeplitz_band(taps, width):
    count = taps.shape[0]
    line = jnp.concatenate([taps, jnp.zeros((width,), taps.dtype)])
    flat = jnp.tile(line, width)[: width * (count + width - 1)]
    return flat.reshape(width, count + width - 1).T


def gram(a, b):
    return lax.dot_general(a, b, (((1,), (1,)), ((), ())), preferred_element_type=jnp.float32)


def orthonormal_rows(image, rows):
    result = image
    for i in range(image.shape[0]):
        row = result[i : i + 1, :]
        unit = row / jnp.sqrt(jnp.sum(row * row, axis=1, keepdims=True))
        proj = jnp.sum(result * unit, axis=1, keepdims=True)
        result = jnp.where(rows > i, result - proj * unit, jnp.where(rows == i, unit, result))
    return result


def subspace_kernel(band_ref, start_ref, out_ref):
    windows = out_ref.shape[0]
    rank, win = start_ref.shape
    rows = lax.broadcasted_iota(jnp.int32, (rank, 1), 0)
    bases = [start_ref[...] for _ in range(windows)]
    for sweep in range(ITERS):
        for number in range(windows):
            lo = number * STRIDE
            scatter_mat = band_ref[lo : lo + win, lo : lo + win]
            image = jnp.dot(
                bases[number], scatter_mat, precision=lax.Precision.HIGHEST,
                preferred_element_type=jnp.float32,
            )
            bases[number] = orthonormal_rows(image, rows)
    for number in range(windows):
        out_ref[number] = bases[number].astype(out_ref.dtype)


def subspace(band, start_t, windows):
    return pl.pallas_call(
        subspace_kernel,
        out_shape=jax.ShapeDtypeStruct((windows,) + start_t.shape, jnp.bfloat16),
        in_specs=[
            pl.BlockSpec(memory_space=pltpu.VMEM),
            pl.BlockSpec(memory_space=pltpu.VMEM),
        ],
        out_specs=pl.BlockSpec(memory_space=pltpu.VMEM),
    )(band, start_t)


def fir_kernel(head_ref, tail_ref, top_ref, rest_ref, out_ref):
    out_ref[...] = jnp.dot(
        head_ref[...], top_ref[...], preferred_element_type=jnp.float32
    ) + jnp.dot(tail_ref[...], rest_ref[...], preferred_element_type=jnp.float32)


def fir(padded, fir_taps, chans, samples):
    width = math.gcd(samples, 512)
    edge = TAPS - 1
    band = toeplitz_band(fir_taps, width)
    top, rest = band[:width], band[width:]
    step = width // edge
    return pl.pallas_call(
        fir_kernel,
        grid=(samples // width,),
        out_shape=jax.ShapeDtypeStruct((chans, samples), jnp.float32),
        in_specs=[
            pl.BlockSpec((chans, width), lambda b: (0, b)),
            pl.BlockSpec((chans, edge), lambda b: (0, (b + 1) * step)),
            pl.BlockSpec((width, width), lambda b: (0, 0)),
            pl.BlockSpec((edge, width), lambda b: (0, 0)),
        ],
        out_specs=pl.BlockSpec((chans, width), lambda b: (0, b)),
    )(padded, padded, top, rest)


def ta_sum(value):
    count = lax.axis_size("ta")
    if count != 4:
        return lax.psum(value, "ta")
    core = lax.axis_index("ta") % 2
    rows = value.shape[0] // 2
    low, high = value[:rows], value[rows:]
    mine = jnp.where(core == 0, low, high)
    theirs = jnp.where(core == 0, high, low)
    partner = [(i, i ^ 1) for i in range(count)]
    across = [(i, i ^ 2) for i in range(count)]
    part = mine + lax.ppermute(theirs, "ta", partner)
    part = part + lax.ppermute(part, "ta", across)
    other = lax.ppermute(part, "ta", partner)
    return jnp.where(core == 0, jnp.concatenate([part, other]), jnp.concatenate([other, part]))


def per_device(raw, fir_taps, start_basis):
    chans = raw.shape[0]
    samples = raw.shape[1]
    half = (TAPS - 1) // 2
    padded = with_halo(raw, (("ta", 1),), half)
    filtered = fir(padded, fir_taps, chans, samples)
    extended = with_halo(filtered, (("ch", 0),), GAUGE)
    gauged = (extended[2 * GAUGE :] - extended[: -2 * GAUGE]).astype(jnp.bfloat16)

    tiles = chans // STRIDE
    windows = tiles
    total_time = samples * lax.axis_size("ta")
    lower_part = shifted(gauged[chans - 2 * STRIDE :], "ch", 1)
    upper_part = shifted(gauged[:STRIDE], "ch", -1)

    own = ta_sum(gram(gauged, gauged))
    own_left = shifted(own[chans - 2 * STRIDE :, chans - 2 * STRIDE :], "ch", 1)
    own_right = shifted(own[:STRIDE, :STRIDE], "ch", -1)

    own, lower_part, upper_part = lax.optimization_barrier((own, lower_part, upper_part))
    cross_left = gram(lower_part, gauged)
    tail = jnp.concatenate([lower_part[STRIDE:], gauged], axis=0)
    cross_right = gram(tail, upper_part)
    packed = ta_sum(jnp.concatenate([cross_left[:, :STRIDE], cross_left[:, STRIDE:], cross_right], axis=0))
    tiles_left = lower_part.shape[0]
    cross_left = jnp.concatenate(
        [packed[:tiles_left], packed[tiles_left : 2 * tiles_left]], axis=1
    )
    cross_right = packed[2 * tiles_left :]

    zeros = jnp.zeros((STRIDE, STRIDE), jnp.float32)
    top = jnp.concatenate(
        [own_left, cross_left, jnp.concatenate([zeros, cross_right[:STRIDE]], axis=0)], axis=1
    )
    middle = jnp.concatenate(
        [cross_left.T, own, cross_right[STRIDE:]], axis=1
    )
    corner = jnp.concatenate([zeros, cross_right[:STRIDE].T], axis=1)
    bottom = jnp.concatenate([corner, cross_right[STRIDE:].T, own_right], axis=1)
    band = jnp.concatenate([top, middle, bottom], axis=0) / total_time

    rounded = subspace(band, start_basis.T, windows)

    stacked = jnp.concatenate([lower_part, gauged, upper_part], axis=0)
    outputs = []
    for number in range(windows):
        frame = stacked[number * STRIDE : number * STRIDE + WIN]
        coeffs = jnp.dot(rounded[number], frame, preferred_element_type=jnp.float32).astype(
            jnp.bfloat16
        )
        fitted = lax.dot_general(
            rounded[number, :, 2 * STRIDE : 3 * STRIDE], coeffs, (((0,), (0,)), ((), ())),
            preferred_element_type=jnp.float32,
        )
        outputs.append(
            (frame[2 * STRIDE : 3 * STRIDE].astype(jnp.float32) - fitted).astype(jnp.bfloat16)
        )
    return jnp.concatenate(outputs, axis=0)


def solution(mesh):
    return jax.shard_map(
        per_device,
        mesh=mesh,
        in_specs=(P("ch", "ta"), P(), P()),
        out_specs=P("ch", "ta"),
        check_vma=False,
    )
```

```python
import math

import jax
import jax.numpy as jnp
from jax import lax
from jax.experimental import pallas as pl
from jax.experimental.pallas import tpu as pltpu
from jax.sharding import PartitionSpec as P

TAPS = 129
GAUGE = 4
STRIDE = 128
RANK = 16
ITERS = 6
WIN = 512


def with_halo(block, sides, width):
    for axis, dim in sides:
        count = lax.axis_size(axis)
        forward = [(i, i + 1) for i in range(count - 1)]
        backward = [(target, source) for source, target in forward]
        low = lax.ppermute(
            lax.slice_in_dim(block, block.shape[dim] - width, None, axis=dim), axis, forward
        )
        high = lax.ppermute(lax.slice_in_dim(block, 0, width, axis=dim), axis, backward)
        block = jnp.concatenate([low, block, high], axis=dim)
    return block


def shifted(value, axis, steps):
    count = lax.axis_size(axis)
    first, last = (max(0, -steps), min(count, count - steps))
    return lax.ppermute(value, axis, [(source, source + steps) for source in range(first, last)])


def toeplitz_band(taps, width):
    count = taps.shape[0]
    line = jnp.concatenate([taps, jnp.zeros((width,), taps.dtype)])
    flat = jnp.tile(line, width)[: width * (count + width - 1)]
    return flat.reshape(width, count + width - 1).T


def gram(a, b):
    return lax.dot_general(a, b, (((1,), (1,)), ((), ())), preferred_element_type=jnp.float32)


def orthonormal_rows(image, rows):
    result = image
    for i in range(image.shape[0]):
        row = result[i : i + 1, :]
        unit = row / jnp.sqrt(jnp.sum(row * row, axis=1, keepdims=True))
        proj = jnp.sum(result * unit, axis=1, keepdims=True)
        result = jnp.where(rows > i, result - proj * unit, jnp.where(rows == i, unit, result))
    return result


def subspace_kernel(band_ref, start_ref, out_ref):
    windows = out_ref.shape[0]
    rank, win = start_ref.shape
    rows = lax.broadcasted_iota(jnp.int32, (rank, 1), 0)
    bases = [start_ref[...] for _ in range(windows)]
    for sweep in range(ITERS):
        for number in range(windows):
            lo = number * STRIDE
            scatter_mat = band_ref[lo : lo + win, lo : lo + win]
            image = jnp.dot(
                bases[number], scatter_mat, precision=lax.Precision.HIGHEST,
                preferred_element_type=jnp.float32,
            )
            bases[number] = orthonormal_rows(image, rows)
    for number in range(windows):
        out_ref[number] = bases[number].astype(out_ref.dtype)


def subspace(band, start_t, windows):
    return pl.pallas_call(
        subspace_kernel,
        out_shape=jax.ShapeDtypeStruct((windows,) + start_t.shape, jnp.bfloat16),
        in_specs=[
            pl.BlockSpec(memory_space=pltpu.VMEM),
            pl.BlockSpec(memory_space=pltpu.VMEM),
        ],
        out_specs=pl.BlockSpec(memory_space=pltpu.VMEM),
    )(band, start_t)


def fir_kernel(head_ref, tail_ref, top_ref, rest_ref, out_ref):
    out_ref[...] = jnp.dot(
        head_ref[...], top_ref[...], preferred_element_type=jnp.float32
    ) + jnp.dot(tail_ref[...], rest_ref[...], preferred_element_type=jnp.float32)


def fir(padded, fir_taps, chans, samples, start):
    width = math.gcd(math.gcd(samples, start) if start else samples, 512)
    first = start // width
    edge = TAPS - 1
    band = toeplitz_band(fir_taps, width)
    top, rest = band[:width], band[width:]
    step = width // edge
    return pl.pallas_call(
        fir_kernel,
        grid=(samples // width,),
        out_shape=jax.ShapeDtypeStruct((chans, samples), jnp.float32),
        in_specs=[
            pl.BlockSpec((chans, width), lambda b: (0, b + first)),
            pl.BlockSpec((chans, edge), lambda b: (0, (b + first + 1) * step)),
            pl.BlockSpec((width, width), lambda b: (0, 0)),
            pl.BlockSpec((edge, width), lambda b: (0, 0)),
        ],
        out_specs=pl.BlockSpec((chans, width), lambda b: (0, b)),
    )(padded, padded, top, rest)


def clean_kernel(lower_ref, own_ref, upper_ref, basis_ref, middle_ref, out_ref):
    tiles = own_ref.shape[0] // STRIDE
    parts = [lower_ref[k * STRIDE : (k + 1) * STRIDE] for k in range(2)]
    parts += [own_ref[k * STRIDE : (k + 1) * STRIDE] for k in range(tiles)]
    parts.append(upper_ref[...])
    for number in range(tiles):
        coeffs = jnp.dot(basis_ref[number, :, 0:STRIDE], parts[number], preferred_element_type=jnp.float32)
        for k in range(1, WIN // STRIDE):
            coeffs = coeffs + jnp.dot(
                basis_ref[number, :, k * STRIDE : (k + 1) * STRIDE], parts[number + k],
                preferred_element_type=jnp.float32,
            )
        fitted = jnp.dot(
            middle_ref[number], coeffs.astype(jnp.bfloat16), preferred_element_type=jnp.float32
        )
        out_ref[number * STRIDE : (number + 1) * STRIDE] = (
            parts[number + 2].astype(jnp.float32) - fitted
        ).astype(out_ref.dtype)


def clean(lower, own, upper, rounded):
    chans, samples = own.shape
    width = math.gcd(samples, 512)
    middle = jnp.swapaxes(rounded[:, :, 2 * STRIDE : 3 * STRIDE], 1, 2)
    return pl.pallas_call(
        clean_kernel,
        grid=(samples // width,),
        out_shape=jax.ShapeDtypeStruct((chans, samples), own.dtype),
        in_specs=[
            pl.BlockSpec((lower.shape[0], width), lambda b: (0, b)),
            pl.BlockSpec((chans, width), lambda b: (0, b)),
            pl.BlockSpec((STRIDE, width), lambda b: (0, b)),
            pl.BlockSpec(rounded.shape, lambda b: (0, 0, 0)),
            pl.BlockSpec(middle.shape, lambda b: (0, 0, 0)),
        ],
        out_specs=pl.BlockSpec((chans, width), lambda b: (0, b)),
    )(lower, own, upper, rounded, middle)


def ta_sum(value):
    count = lax.axis_size("ta")
    if count != 4:
        return lax.psum(value, "ta")
    core = lax.axis_index("ta") % 2
    rows = value.shape[0] // 2
    low, high = value[:rows], value[rows:]
    mine = jnp.where(core == 0, low, high)
    theirs = jnp.where(core == 0, high, low)
    partner = [(i, i ^ 1) for i in range(count)]
    across = [(i, i ^ 2) for i in range(count)]
    part = mine + lax.ppermute(theirs, "ta", partner)
    part = part + lax.ppermute(part, "ta", across)
    other = lax.ppermute(part, "ta", partner)
    return jnp.where(core == 0, jnp.concatenate([part, other]), jnp.concatenate([other, part]))


def per_device(raw, fir_taps, start_basis):
    chans = raw.shape[0]
    samples = raw.shape[1]
    half = (TAPS - 1) // 2
    padded = with_halo(raw, (("ta", 1),), half)
    chunks = 2 if samples % 1024 == 0 else 1
    piece = samples // chunks
    tiles = chans // STRIDE
    windows = tiles
    total_time = samples * lax.axis_size("ta")
    gaugeds, lowers, uppers = [], [], []
    own = cross_left = cross_right = None
    for number in range(chunks):
        filtered = fir(padded, fir_taps, chans, piece, number * piece)
        extended = with_halo(filtered, (("ch", 0),), GAUGE)
        gauged = (extended[2 * GAUGE :] - extended[: -2 * GAUGE]).astype(jnp.bfloat16)
        lower_part = shifted(gauged[chans - 2 * STRIDE :], "ch", 1)
        upper_part = shifted(gauged[:STRIDE], "ch", -1)
        local = gram(gauged, gauged)
        own = local if own is None else own + local
        gaugeds.append(gauged)
        lowers.append(lower_part)
        uppers.append(upper_part)

    own = ta_sum(own)
    own_left = shifted(own[chans - 2 * STRIDE :, chans - 2 * STRIDE :], "ch", 1)
    own_right = shifted(own[:STRIDE, :STRIDE], "ch", -1)
    own, lowers, uppers = lax.optimization_barrier((own, lowers, uppers))

    for number in range(chunks):
        lower_part, gauged, upper_part = lowers[number], gaugeds[number], uppers[number]
        left = gram(lower_part, gauged)
        tail = jnp.concatenate([lower_part[STRIDE:], gauged], axis=0)
        right = gram(tail, upper_part)
        cross_left = left if cross_left is None else cross_left + left
        cross_right = right if cross_right is None else cross_right + right

    packed = ta_sum(jnp.concatenate([cross_left[:, :STRIDE], cross_left[:, STRIDE:], cross_right], axis=0))
    tiles_left = 2 * STRIDE
    cross_left = jnp.concatenate(
        [packed[:tiles_left], packed[tiles_left : 2 * tiles_left]], axis=1
    )
    cross_right = packed[2 * tiles_left :]

    zeros = jnp.zeros((STRIDE, STRIDE), jnp.float32)
    top = jnp.concatenate(
        [own_left, cross_left, jnp.concatenate([zeros, cross_right[:STRIDE]], axis=0)], axis=1
    )
    middle = jnp.concatenate(
        [cross_left.T, own, cross_right[STRIDE:]], axis=1
    )
    corner = jnp.concatenate([zeros, cross_right[:STRIDE].T], axis=1)
    bottom = jnp.concatenate([corner, cross_right[STRIDE:].T, own_right], axis=1)
    band = jnp.concatenate([top, middle, bottom], axis=0) / total_time

    rounded = subspace(band, start_basis.T, windows)
    outputs = [
        clean(lowers[number], gaugeds[number], uppers[number], rounded) for number in range(chunks)
    ]
    return jnp.concatenate(outputs, axis=1)


def solution(mesh):
    return jax.shard_map(
        per_device,
        mesh=mesh,
        in_specs=(P("ch", "ta"), P(), P()),
        out_specs=P("ch", "ta"),
        check_vma=False,
    )
```

```python
import math

import jax
import jax.numpy as jnp
from jax import lax
from jax.experimental import pallas as pl
from jax.experimental.pallas import tpu as pltpu
from jax.sharding import PartitionSpec as P

TAPS = 129
GAUGE = 4
STRIDE = 128
RANK = 16
ITERS = 6
WIN = 512


def with_halo(block, sides, width):
    for axis, dim in sides:
        count = lax.axis_size(axis)
        forward = [(i, i + 1) for i in range(count - 1)]
        backward = [(target, source) for source, target in forward]
        low = lax.ppermute(
            lax.slice_in_dim(block, block.shape[dim] - width, None, axis=dim), axis, forward
        )
        high = lax.ppermute(lax.slice_in_dim(block, 0, width, axis=dim), axis, backward)
        block = jnp.concatenate([low, block, high], axis=dim)
    return block


def shifted(value, axis, steps):
    count = lax.axis_size(axis)
    first, last = (max(0, -steps), min(count, count - steps))
    return lax.ppermute(value, axis, [(source, source + steps) for source in range(first, last)])


def toeplitz_band(taps, width):
    count = taps.shape[0]
    line = jnp.concatenate([taps, jnp.zeros((width,), taps.dtype)])
    flat = jnp.tile(line, width)[: width * (count + width - 1)]
    return flat.reshape(width, count + width - 1).T


def gram(a, b):
    return lax.dot_general(a, b, (((1,), (1,)), ((), ())), preferred_element_type=jnp.float32)


def orthonormal_rows(image, rows):
    result = image
    for i in range(image.shape[0]):
        row = result[i : i + 1, :]
        unit = row / jnp.sqrt(jnp.sum(row * row, axis=1, keepdims=True))
        proj = jnp.sum(result * unit, axis=1, keepdims=True)
        result = jnp.where(rows > i, result - proj * unit, jnp.where(rows == i, unit, result))
    return result


def subspace_kernel(band_ref, start_ref, out_ref):
    windows = out_ref.shape[0]
    rank, win = start_ref.shape
    rows = lax.broadcasted_iota(jnp.int32, (rank, 1), 0)
    bases = [start_ref[...] for _ in range(windows)]
    for sweep in range(ITERS):
        for number in range(windows):
            lo = number * STRIDE
            scatter_mat = band_ref[lo : lo + win, lo : lo + win]
            image = jnp.dot(
                bases[number], scatter_mat, precision=lax.Precision.HIGHEST,
                preferred_element_type=jnp.float32,
            )
            bases[number] = orthonormal_rows(image, rows)
    for number in range(windows):
        out_ref[number] = bases[number].astype(out_ref.dtype)


def subspace(band, start_t, windows):
    return pl.pallas_call(
        subspace_kernel,
        out_shape=jax.ShapeDtypeStruct((windows,) + start_t.shape, jnp.bfloat16),
        in_specs=[
            pl.BlockSpec(memory_space=pltpu.VMEM),
            pl.BlockSpec(memory_space=pltpu.VMEM),
        ],
        out_specs=pl.BlockSpec(memory_space=pltpu.VMEM),
    )(band, start_t)


def fir_kernel(left_ref, right_ref, prev_ref, cur_ref, next_ref, lo_ref, mid_ref, hi_ref, out_ref, *, first, last):
    block = pl.program_id(0) + first
    before = jnp.where(block == 0, left_ref[...], prev_ref[...])
    after = jnp.where(block == last, right_ref[...], next_ref[...])
    out_ref[...] = (
        jnp.dot(before, lo_ref[...], preferred_element_type=jnp.float32)
        + jnp.dot(cur_ref[...], mid_ref[...], preferred_element_type=jnp.float32)
        + jnp.dot(after, hi_ref[...], preferred_element_type=jnp.float32)
    )


def fir(raw, left, right, band, start, length):
    chans, samples = raw.shape
    width = band.shape[1]
    edge = 128
    step = width // edge
    first = start // width
    lo, mid, hi = band[:edge], band[edge : edge + width], band[edge + width :]
    kernel = lambda *refs: fir_kernel(*refs, first=first, last=samples // width - 1)
    full = lambda b: (0, 0)
    return pl.pallas_call(
        kernel,
        grid=(length // width,),
        out_shape=jax.ShapeDtypeStruct((chans, length), jnp.float32),
        in_specs=[
            pl.BlockSpec((chans, edge), full),
            pl.BlockSpec((chans, edge), full),
            pl.BlockSpec((chans, edge), lambda b: (0, jnp.maximum((b + first) * step - 1, 0))),
            pl.BlockSpec((chans, width), lambda b: (0, b + first)),
            pl.BlockSpec(
                (chans, edge), lambda b: (0, jnp.minimum((b + first + 1) * step, samples // edge - 1))
            ),
            pl.BlockSpec((edge, width), full),
            pl.BlockSpec((width, width), full),
            pl.BlockSpec((edge, width), full),
        ],
        out_specs=pl.BlockSpec((chans, width), lambda b: (0, b)),
    )(left, right, raw, raw, raw, lo, mid, hi)


def clean_kernel(lower_ref, own_ref, upper_ref, basis_ref, middle_ref, *rest):
    out_ref = rest[-1]
    tiles = own_ref.shape[0] // STRIDE
    parts = [lower_ref[k * STRIDE : (k + 1) * STRIDE] for k in range(2)]
    parts += [own_ref[k * STRIDE : (k + 1) * STRIDE] for k in range(tiles)]
    parts.append(upper_ref[...])
    for number in range(tiles):
        coeffs = jnp.dot(basis_ref[number, :, 0:STRIDE], parts[number], preferred_element_type=jnp.float32)
        for k in range(1, WIN // STRIDE):
            coeffs = coeffs + jnp.dot(
                basis_ref[number, :, k * STRIDE : (k + 1) * STRIDE], parts[number + k],
                preferred_element_type=jnp.float32,
            )
        fitted = jnp.dot(
            middle_ref[number], coeffs.astype(jnp.bfloat16), preferred_element_type=jnp.float32
        )
        out_ref[number * STRIDE : (number + 1) * STRIDE] = (
            parts[number + 2].astype(jnp.float32) - fitted
        ).astype(out_ref.dtype)


def clean(lower, own, upper, rounded, total, start, into):
    chans, samples = own.shape
    width = math.gcd(math.gcd(samples, start) if start else samples, 512)
    first = start // width
    middle = jnp.swapaxes(rounded[:, :, 2 * STRIDE : 3 * STRIDE], 1, 2)
    return pl.pallas_call(
        clean_kernel,
        grid=(samples // width,),
        out_shape=jax.ShapeDtypeStruct((chans, total), own.dtype),
        in_specs=[
            pl.BlockSpec((lower.shape[0], width), lambda b: (0, b)),
            pl.BlockSpec((chans, width), lambda b: (0, b)),
            pl.BlockSpec((STRIDE, width), lambda b: (0, b)),
            pl.BlockSpec(rounded.shape, lambda b: (0, 0, 0)),
            pl.BlockSpec(middle.shape, lambda b: (0, 0, 0)),
        ] + ([] if into is None else [pl.BlockSpec(memory_space=pl.ANY)]),
        out_specs=pl.BlockSpec((chans, width), lambda b: (0, b + first)),
        input_output_aliases={} if into is None else {5: 0},
    )(lower, own, upper, rounded, middle, *([] if into is None else [into]))


def ta_sum(value):
    count = lax.axis_size("ta")
    if count != 4:
        return lax.psum(value, "ta")
    core = lax.axis_index("ta") % 2
    rows = value.shape[0] // 2
    low, high = value[:rows], value[rows:]
    mine = jnp.where(core == 0, low, high)
    theirs = jnp.where(core == 0, high, low)
    partner = [(i, i ^ 1) for i in range(count)]
    across = [(i, i ^ 2) for i in range(count)]
    part = mine + lax.ppermute(theirs, "ta", partner)
    part = part + lax.ppermute(part, "ta", across)
    other = lax.ppermute(part, "ta", partner)
    return jnp.where(core == 0, jnp.concatenate([part, other]), jnp.concatenate([other, part]))


def per_device(raw, fir_taps, start_basis):
    chans = raw.shape[0]
    samples = raw.shape[1]
    half = (TAPS - 1) // 2
    count = lax.axis_size("ta")
    forward = [(i, i + 1) for i in range(count - 1)]
    backward = [(target, source) for source, target in forward]
    blank = jnp.zeros((chans, STRIDE - half), raw.dtype)
    left = jnp.concatenate([blank, lax.ppermute(raw[:, samples - half :], "ta", forward)], axis=1)
    right = jnp.concatenate([lax.ppermute(raw[:, :half], "ta", backward), blank], axis=1)
    width = math.gcd(samples, 512)
    band = jnp.pad(toeplitz_band(fir_taps, width), ((half, half), (0, 0)))
    source = raw
    chunks = 2 if samples % 1024 == 0 else 1
    piece = samples // chunks
    tiles = chans // STRIDE
    windows = tiles
    total_time = samples * lax.axis_size("ta")
    gaugeds, lowers, uppers = [], [], []
    own = cross_left = cross_right = None
    for number in range(chunks):
        filtered = fir(source, left, right, band, number * piece, piece)
        extended = with_halo(filtered, (("ch", 0),), GAUGE)
        gauged = (extended[2 * GAUGE :] - extended[: -2 * GAUGE]).astype(jnp.bfloat16)
        lower_part = shifted(gauged[chans - 2 * STRIDE :], "ch", 1)
        upper_part = shifted(gauged[:STRIDE], "ch", -1)
        local = gram(gauged, gauged)
        own = local if own is None else own + local
        gaugeds.append(gauged)
        source, gauged = lax.optimization_barrier((source, gauged))
        lowers.append(lower_part)
        uppers.append(upper_part)

    own = ta_sum(own)
    own_left = shifted(own[chans - 2 * STRIDE :, chans - 2 * STRIDE :], "ch", 1)
    own_right = shifted(own[:STRIDE, :STRIDE], "ch", -1)
    own, lowers, uppers = lax.optimization_barrier((own, lowers, uppers))

    for number in range(chunks):
        lower_part, gauged, upper_part = lowers[number], gaugeds[number], uppers[number]
        left = gram(lower_part, gauged)
        tail = jnp.concatenate([lower_part[STRIDE:], gauged], axis=0)
        right = gram(tail, upper_part)
        cross_left = left if cross_left is None else cross_left + left
        cross_right = right if cross_right is None else cross_right + right

    packed = ta_sum(jnp.concatenate([cross_left[:, :STRIDE], cross_left[:, STRIDE:], cross_right], axis=0))
    tiles_left = 2 * STRIDE
    cross_left = jnp.concatenate(
        [packed[:tiles_left], packed[tiles_left : 2 * tiles_left]], axis=1
    )
    cross_right = packed[2 * tiles_left :]

    zeros = jnp.zeros((STRIDE, STRIDE), jnp.float32)
    top = jnp.concatenate(
        [own_left, cross_left, jnp.concatenate([zeros, cross_right[:STRIDE]], axis=0)], axis=1
    )
    middle = jnp.concatenate(
        [cross_left.T, own, cross_right[STRIDE:]], axis=1
    )
    corner = jnp.concatenate([zeros, cross_right[:STRIDE].T], axis=1)
    bottom = jnp.concatenate([corner, cross_right[STRIDE:].T, own_right], axis=1)
    band = jnp.concatenate([top, middle, bottom], axis=0) / total_time

    rounded = subspace(band, start_basis.T, windows)
    cleaned = None
    for number in range(chunks):
        cleaned = clean(
            lowers[number], gaugeds[number], uppers[number], rounded, samples, number * piece, cleaned
        )
    return cleaned


def solution(mesh):
    return jax.shard_map(
        per_device,
        mesh=mesh,
        in_specs=(P("ch", "ta"), P(), P()),
        out_specs=P("ch", "ta"),
        check_vma=False,
    )
```

```python
import math

import jax
import jax.numpy as jnp
from jax import lax
from jax.experimental import pallas as pl
from jax.experimental.pallas import tpu as pltpu
from jax.sharding import PartitionSpec as P


TAPS = 129
GAUGE = 4
STRIDE = 128
RANK = 16
ITERS = 6
WIN = 512


def with_halo(block, sides, width):
    for axis, dim in sides:
        count = lax.axis_size(axis)
        forward = [(i, i + 1) for i in range(count - 1)]
        backward = [(target, source) for source, target in forward]
        low = lax.ppermute(
            lax.slice_in_dim(block, block.shape[dim] - width, None, axis=dim), axis, forward
        )
        high = lax.ppermute(lax.slice_in_dim(block, 0, width, axis=dim), axis, backward)
        block = jnp.concatenate([low, block, high], axis=dim)
    return block


def shifted(value, axis, steps):
    count = lax.axis_size(axis)
    first, last = (max(0, -steps), min(count, count - steps))
    return lax.ppermute(value, axis, [(source, source + steps) for source in range(first, last)])


def toeplitz_band(taps, width):
    count = taps.shape[0]
    line = jnp.concatenate([taps, jnp.zeros((width,), taps.dtype)])
    flat = jnp.tile(line, width)[: width * (count + width - 1)]
    return flat.reshape(width, count + width - 1).T


def gram(a, b):
    return lax.dot_general(a, b, (((1,), (1,)), ((), ())), preferred_element_type=jnp.float32)


def orthonormal_rows(image, rows):
    result = image
    for i in range(image.shape[0]):
        row = result[i : i + 1, :]
        unit = row / jnp.sqrt(jnp.sum(row * row, axis=1, keepdims=True))
        proj = jnp.sum(result * unit, axis=1, keepdims=True)
        result = jnp.where(rows > i, result - proj * unit, jnp.where(rows == i, unit, result))
    return result


def subspace_kernel(band_ref, start_ref, out_ref):
    windows = out_ref.shape[0]
    rank, win = start_ref.shape
    rows = lax.broadcasted_iota(jnp.int32, (rank, 1), 0)
    bases = [start_ref[...] for _ in range(windows)]
    for sweep in range(ITERS):
        for number in range(windows):
            lo = number * STRIDE
            scatter_mat = band_ref[lo : lo + win, lo : lo + win]
            image = jnp.dot(
                bases[number], scatter_mat, precision=lax.Precision.HIGHEST,
                preferred_element_type=jnp.float32,
            )
            bases[number] = orthonormal_rows(image, rows)
    for number in range(windows):
        out_ref[number] = bases[number].astype(out_ref.dtype)


def subspace(band, start_t, windows):
    return pl.pallas_call(
        subspace_kernel,
        out_shape=jax.ShapeDtypeStruct((windows,) + start_t.shape, jnp.bfloat16),
        in_specs=[
            pl.BlockSpec(memory_space=pltpu.VMEM),
            pl.BlockSpec(memory_space=pltpu.VMEM),
        ],
        out_specs=pl.BlockSpec(memory_space=pltpu.VMEM),
    )(band, start_t)


def fir_kernel(left_ref, right_ref, prev_ref, cur_ref, next_ref, lo_ref, mid_ref, hi_ref, out_ref, *, first, last):
    block = pl.program_id(0) + first
    before = jnp.where(block == 0, left_ref[...], prev_ref[...])
    after = jnp.where(block == last, right_ref[...], next_ref[...])
    out_ref[...] = (
        jnp.dot(before, lo_ref[...], preferred_element_type=jnp.float32)
        + jnp.dot(cur_ref[...], mid_ref[...], preferred_element_type=jnp.float32)
        + jnp.dot(after, hi_ref[...], preferred_element_type=jnp.float32)
    )


def fir(raw, left, right, band, start, length):
    chans, samples = raw.shape
    width = band.shape[1]
    edge = 128
    step = width // edge
    first = start // width
    lo, mid, hi = band[:edge], band[edge : edge + width], band[edge + width :]
    kernel = lambda *refs: fir_kernel(*refs, first=first, last=samples // width - 1)
    full = lambda b: (0, 0)
    return pl.pallas_call(
        kernel,
        grid=(length // width,),
        out_shape=jax.ShapeDtypeStruct((chans, length), jnp.float32),
        in_specs=[
            pl.BlockSpec((chans, edge), full),
            pl.BlockSpec((chans, edge), full),
            pl.BlockSpec((chans, edge), lambda b: (0, jnp.maximum((b + first) * step - 1, 0))),
            pl.BlockSpec((chans, width), lambda b: (0, b + first)),
            pl.BlockSpec(
                (chans, edge), lambda b: (0, jnp.minimum((b + first + 1) * step, samples // edge - 1))
            ),
            pl.BlockSpec((edge, width), full),
            pl.BlockSpec((width, width), full),
            pl.BlockSpec((edge, width), full),
        ],
        out_specs=pl.BlockSpec((chans, width), lambda b: (0, b)),
    )(left, right, raw, raw, raw, lo, mid, hi)


def clean_kernel(lower_ref, own_ref, upper_ref, basis_ref, middle_ref, *rest):
    out_ref = rest[-1]
    tiles = own_ref.shape[0] // STRIDE
    parts = [lower_ref[k * STRIDE : (k + 1) * STRIDE] for k in range(2)]
    parts += [own_ref[k * STRIDE : (k + 1) * STRIDE] for k in range(tiles)]
    parts.append(upper_ref[...])
    for number in range(tiles):
        coeffs = jnp.dot(basis_ref[number, :, 0:STRIDE], parts[number], preferred_element_type=jnp.float32)
        for k in range(1, WIN // STRIDE):
            coeffs = coeffs + jnp.dot(
                basis_ref[number, :, k * STRIDE : (k + 1) * STRIDE], parts[number + k],
                preferred_element_type=jnp.float32,
            )
        fitted = jnp.dot(
            middle_ref[number], coeffs.astype(jnp.bfloat16), preferred_element_type=jnp.float32
        )
        out_ref[number * STRIDE : (number + 1) * STRIDE] = (
            parts[number + 2].astype(jnp.float32) - fitted
        ).astype(out_ref.dtype)


def clean(lower, own, upper, rounded, total, start, into):
    chans, samples = own.shape
    width = math.gcd(math.gcd(samples, start) if start else samples, 512)
    first = start // width
    middle = jnp.swapaxes(rounded[:, :, 2 * STRIDE : 3 * STRIDE], 1, 2)
    return pl.pallas_call(
        clean_kernel,
        grid=(samples // width,),
        out_shape=jax.ShapeDtypeStruct((chans, total), own.dtype),
        in_specs=[
            pl.BlockSpec((lower.shape[0], width), lambda b: (0, b)),
            pl.BlockSpec((chans, width), lambda b: (0, b)),
            pl.BlockSpec((STRIDE, width), lambda b: (0, b)),
            pl.BlockSpec(rounded.shape, lambda b: (0, 0, 0)),
            pl.BlockSpec(middle.shape, lambda b: (0, 0, 0)),
        ] + ([] if into is None else [pl.BlockSpec(memory_space=pl.ANY)]),
        out_specs=pl.BlockSpec((chans, width), lambda b: (0, b + first)),
        input_output_aliases={} if into is None else {5: 0},
    )(lower, own, upper, rounded, middle, *([] if into is None else [into]))


def ta_sum(value):
    count = lax.axis_size("ta")
    if count != 4:
        return lax.psum(value, "ta")
    core = lax.axis_index("ta") % 2
    rows = value.shape[0] // 2
    low, high = value[:rows], value[rows:]
    mine = jnp.where(core == 0, low, high)
    theirs = jnp.where(core == 0, high, low)
    partner = [(i, i ^ 1) for i in range(count)]
    across = [(i, i ^ 2) for i in range(count)]
    part = mine + lax.ppermute(theirs, "ta", partner)
    part = part + lax.ppermute(part, "ta", across)
    other = lax.ppermute(part, "ta", partner)
    return jnp.where(core == 0, jnp.concatenate([part, other]), jnp.concatenate([other, part]))


def per_device(raw, fir_taps, start_basis):
    chans = raw.shape[0]
    samples = raw.shape[1]
    half = (TAPS - 1) // 2
    count = lax.axis_size("ta")
    forward = [(i, i + 1) for i in range(count - 1)]
    backward = [(target, source) for source, target in forward]
    blank = jnp.zeros((chans, STRIDE - half), raw.dtype)
    left = jnp.concatenate([blank, lax.ppermute(raw[:, samples - half :], "ta", forward)], axis=1)
    right = jnp.concatenate([lax.ppermute(raw[:, :half], "ta", backward), blank], axis=1)
    width = math.gcd(samples, 512)
    band = jnp.pad(toeplitz_band(fir_taps, width), ((half, half), (0, 0)))
    source = raw
    chunks = 2 if samples % 1024 == 0 else 1
    piece = samples // chunks
    tiles = chans // STRIDE
    windows = tiles
    total_time = samples * lax.axis_size("ta")
    gaugeds, lowers, uppers = [], [], []
    own = cross_left = cross_right = None
    for number in range(chunks):
        filtered = fir(source, left, right, band, number * piece, piece)
        extended = with_halo(filtered, (("ch", 0),), GAUGE)
        gauged = (extended[2 * GAUGE :] - extended[: -2 * GAUGE]).astype(jnp.bfloat16)
        lower_part = shifted(gauged[chans - 2 * STRIDE :], "ch", 1)
        upper_part = shifted(gauged[:STRIDE], "ch", -1)
        local = gram(gauged, gauged)
        own = local if own is None else own + local
        gaugeds.append(gauged)
        source, gauged = lax.optimization_barrier((source, gauged))
        lowers.append(lower_part)
        uppers.append(upper_part)

    own = ta_sum(own)
    own_left = shifted(own[chans - 2 * STRIDE :, chans - 2 * STRIDE :], "ch", 1)
    own_right = shifted(own[:STRIDE, :STRIDE], "ch", -1)
    own, own_left, own_right, lowers, uppers = lax.optimization_barrier(
        (own, own_left, own_right, lowers, uppers)
    )

    for number in range(chunks):
        lower_part, gauged, upper_part = lowers[number], gaugeds[number], uppers[number]
        left = gram(lower_part, gauged)
        tail = jnp.concatenate([lower_part[STRIDE:], gauged], axis=0)
        right = gram(tail, upper_part)
        cross_left = left if cross_left is None else cross_left + left
        cross_right = right if cross_right is None else cross_right + right

    packed = ta_sum(jnp.concatenate([cross_left[:, :STRIDE], cross_left[:, STRIDE:], cross_right], axis=0))
    tiles_left = 2 * STRIDE
    cross_left = jnp.concatenate(
        [packed[:tiles_left], packed[tiles_left : 2 * tiles_left]], axis=1
    )
    cross_right = packed[2 * tiles_left :]

    zeros = jnp.zeros((STRIDE, STRIDE), jnp.float32)
    top = jnp.concatenate(
        [own_left, cross_left, jnp.concatenate([zeros, cross_right[:STRIDE]], axis=0)], axis=1
    )
    middle = jnp.concatenate(
        [cross_left.T, own, cross_right[STRIDE:]], axis=1
    )
    corner = jnp.concatenate([zeros, cross_right[:STRIDE].T], axis=1)
    bottom = jnp.concatenate([corner, cross_right[STRIDE:].T, own_right], axis=1)
    band = jnp.concatenate([top, middle, bottom], axis=0) / total_time

    rounded = subspace(band, start_basis.T, windows)
    cleaned = None
    for number in range(chunks):
        cleaned = clean(
            lowers[number], gaugeds[number], uppers[number], rounded, samples, number * piece, cleaned
        )
    return cleaned


def solution(mesh):
    return jax.shard_map(
        per_device,
        mesh=mesh,
        in_specs=(P("ch", "ta"), P(), P()),
        out_specs=P("ch", "ta"),
        check_vma=False,
    )
```

```python
import math

import jax
import jax.numpy as jnp
from jax import lax
from jax.experimental import pallas as pl
from jax.experimental.pallas import tpu as pltpu
from jax.sharding import PartitionSpec as P

TAPS = 129
GAUGE = 4
STRIDE = 128
RANK = 16
ITERS = 6
WIN = 512


def with_halo(block, sides, width):
    for axis, dim in sides:
        count = lax.axis_size(axis)
        forward = [(i, i + 1) for i in range(count - 1)]
        backward = [(target, source) for source, target in forward]
        low = lax.ppermute(
            lax.slice_in_dim(block, block.shape[dim] - width, None, axis=dim), axis, forward
        )
        high = lax.ppermute(lax.slice_in_dim(block, 0, width, axis=dim), axis, backward)
        block = jnp.concatenate([low, block, high], axis=dim)
    return block


def shifted(value, axis, steps):
    count = lax.axis_size(axis)
    first, last = (max(0, -steps), min(count, count - steps))
    return lax.ppermute(value, axis, [(source, source + steps) for source in range(first, last)])


def toeplitz_band(taps, width):
    count = taps.shape[0]
    line = jnp.concatenate([taps, jnp.zeros((width,), taps.dtype)])
    flat = jnp.tile(line, width)[: width * (count + width - 1)]
    return flat.reshape(width, count + width - 1).T


def gram(a, b):
    return lax.dot_general(a, b, (((1,), (1,)), ((), ())), preferred_element_type=jnp.float32)


def orthonormal_rows(image, rows, lanes):
    rank = image.shape[0]
    gram_mat = lax.dot_general(
        image, image, (((1,), (1,)), ((), ())), precision=lax.Precision.HIGHEST,
        preferred_element_type=jnp.float32,
    )
    result = image
    for j in range(rank):
        column = jnp.sum(jnp.where(lanes == j, gram_mat, 0.0), axis=1, keepdims=True)
        scale = 1.0 / jnp.sqrt(column[j : j + 1, :])
        factor = column * scale
        pivot_row = gram_mat[j : j + 1, :] * scale
        image_row = result[j : j + 1, :] * scale
        below = rows > j
        gram_mat = jnp.where(below, gram_mat - factor * pivot_row, gram_mat)
        result = jnp.where(below, result - factor * image_row, jnp.where(rows == j, image_row, result))
    return result


def subspace_kernel(band_ref, start_ref, out_ref):
    windows = out_ref.shape[0]
    rank, win = start_ref.shape
    rows = lax.broadcasted_iota(jnp.int32, (rank, 1), 0)
    lanes = lax.broadcasted_iota(jnp.int32, (rank, rank), 1)
    bases = [start_ref[...] for _ in range(windows)]
    for sweep in range(ITERS):
        for number in range(windows):
            lo = number * STRIDE
            scatter_mat = band_ref[lo : lo + win, lo : lo + win]
            image = jnp.dot(
                bases[number], scatter_mat, precision=lax.Precision.HIGHEST,
                preferred_element_type=jnp.float32,
            )
            bases[number] = orthonormal_rows(image, rows, lanes)
    for number in range(windows):
        out_ref[number] = bases[number].astype(out_ref.dtype)


def subspace(band, start_t, windows):
    return pl.pallas_call(
        subspace_kernel,
        out_shape=jax.ShapeDtypeStruct((windows,) + start_t.shape, jnp.bfloat16),
        in_specs=[
            pl.BlockSpec(memory_space=pltpu.VMEM),
            pl.BlockSpec(memory_space=pltpu.VMEM),
        ],
        out_specs=pl.BlockSpec(memory_space=pltpu.VMEM),
    )(band, start_t)


def fir_kernel(left_ref, right_ref, prev_ref, cur_ref, next_ref, lo_ref, mid_ref, hi_ref, out_ref, *, first, last):
    block = pl.program_id(0) + first
    before = jnp.where(block == 0, left_ref[...], prev_ref[...])
    after = jnp.where(block == last, right_ref[...], next_ref[...])
    out_ref[...] = (
        jnp.dot(before, lo_ref[...], preferred_element_type=jnp.float32)
        + jnp.dot(cur_ref[...], mid_ref[...], preferred_element_type=jnp.float32)
        + jnp.dot(after, hi_ref[...], preferred_element_type=jnp.float32)
    )


def fir(raw, left, right, band, start, length):
    chans, samples = raw.shape
    width = band.shape[1]
    edge = 128
    step = width // edge
    first = start // width
    lo, mid, hi = band[:edge], band[edge : edge + width], band[edge + width :]
    kernel = lambda *refs: fir_kernel(*refs, first=first, last=samples // width - 1)
    full = lambda b: (0, 0)
    return pl.pallas_call(
        kernel,
        grid=(length // width,),
        out_shape=jax.ShapeDtypeStruct((chans, length), jnp.float32),
        in_specs=[
            pl.BlockSpec((chans, edge), full),
            pl.BlockSpec((chans, edge), full),
            pl.BlockSpec((chans, edge), lambda b: (0, jnp.maximum((b + first) * step - 1, 0))),
            pl.BlockSpec((chans, width), lambda b: (0, b + first)),
            pl.BlockSpec(
                (chans, edge), lambda b: (0, jnp.minimum((b + first + 1) * step, samples // edge - 1))
            ),
            pl.BlockSpec((edge, width), full),
            pl.BlockSpec((width, width), full),
            pl.BlockSpec((edge, width), full),
        ],
        out_specs=pl.BlockSpec((chans, width), lambda b: (0, b)),
    )(left, right, raw, raw, raw, lo, mid, hi)


def clean_kernel(lower_ref, own_ref, upper_ref, basis_ref, middle_ref, *rest):
    out_ref = rest[-1]
    tiles = own_ref.shape[0] // STRIDE
    parts = [lower_ref[k * STRIDE : (k + 1) * STRIDE] for k in range(2)]
    parts += [own_ref[k * STRIDE : (k + 1) * STRIDE] for k in range(tiles)]
    parts.append(upper_ref[...])
    for number in range(tiles):
        coeffs = jnp.dot(basis_ref[number, :, 0:STRIDE], parts[number], preferred_element_type=jnp.float32)
        for k in range(1, WIN // STRIDE):
            coeffs = coeffs + jnp.dot(
                basis_ref[number, :, k * STRIDE : (k + 1) * STRIDE], parts[number + k],
                preferred_element_type=jnp.float32,
            )
        fitted = jnp.dot(
            middle_ref[number], coeffs.astype(jnp.bfloat16), preferred_element_type=jnp.float32
        )
        out_ref[number * STRIDE : (number + 1) * STRIDE] = (
            parts[number + 2].astype(jnp.float32) - fitted
        ).astype(out_ref.dtype)


def clean(lower, own, upper, rounded, total, start, into):
    chans, samples = own.shape
    width = math.gcd(math.gcd(samples, start) if start else samples, 512)
    first = start // width
    middle = jnp.swapaxes(rounded[:, :, 2 * STRIDE : 3 * STRIDE], 1, 2)
    return pl.pallas_call(
        clean_kernel,
        grid=(samples // width,),
        out_shape=jax.ShapeDtypeStruct((chans, total), own.dtype),
        in_specs=[
            pl.BlockSpec((lower.shape[0], width), lambda b: (0, b)),
            pl.BlockSpec((chans, width), lambda b: (0, b)),
            pl.BlockSpec((STRIDE, width), lambda b: (0, b)),
            pl.BlockSpec(rounded.shape, lambda b: (0, 0, 0)),
            pl.BlockSpec(middle.shape, lambda b: (0, 0, 0)),
        ] + ([] if into is None else [pl.BlockSpec(memory_space=pl.ANY)]),
        out_specs=pl.BlockSpec((chans, width), lambda b: (0, b + first)),
        input_output_aliases={} if into is None else {5: 0},
    )(lower, own, upper, rounded, middle, *([] if into is None else [into]))


def ta_sum(value):
    count = lax.axis_size("ta")
    if count != 4:
        return lax.psum(value, "ta")
    core = lax.axis_index("ta") % 2
    rows = value.shape[0] // 2
    low, high = value[:rows], value[rows:]
    mine = jnp.where(core == 0, low, high)
    theirs = jnp.where(core == 0, high, low)
    partner = [(i, i ^ 1) for i in range(count)]
    across = [(i, i ^ 2) for i in range(count)]
    part = mine + lax.ppermute(theirs, "ta", partner)
    part = part + lax.ppermute(part, "ta", across)
    other = lax.ppermute(part, "ta", partner)
    return jnp.where(core == 0, jnp.concatenate([part, other]), jnp.concatenate([other, part]))


def per_device(raw, fir_taps, start_basis):
    chans = raw.shape[0]
    samples = raw.shape[1]
    half = (TAPS - 1) // 2
    count = lax.axis_size("ta")
    forward = [(i, i + 1) for i in range(count - 1)]
    backward = [(target, source) for source, target in forward]
    blank = jnp.zeros((chans, STRIDE - half), raw.dtype)
    left = jnp.concatenate([blank, lax.ppermute(raw[:, samples - half :], "ta", forward)], axis=1)
    right = jnp.concatenate([lax.ppermute(raw[:, :half], "ta", backward), blank], axis=1)
    width = math.gcd(samples, 512)
    band = jnp.pad(toeplitz_band(fir_taps, width), ((half, half), (0, 0)))
    source = raw
    chunks = 2 if samples % 1024 == 0 else 1
    piece = samples // chunks
    tiles = chans // STRIDE
    windows = tiles
    total_time = samples * lax.axis_size("ta")
    gaugeds, lowers, uppers = [], [], []
    own = cross_left = cross_right = None
    for number in range(chunks):
        filtered = fir(source, left, right, band, number * piece, piece)
        extended = with_halo(filtered, (("ch", 0),), GAUGE)
        gauged = (extended[2 * GAUGE :] - extended[: -2 * GAUGE]).astype(jnp.bfloat16)
        lower_part = shifted(gauged[chans - 2 * STRIDE :], "ch", 1)
        upper_part = shifted(gauged[:STRIDE], "ch", -1)
        local = gram(gauged, gauged)
        own = local if own is None else own + local
        gaugeds.append(gauged)
        source, gauged = lax.optimization_barrier((source, gauged))
        lowers.append(lower_part)
        uppers.append(upper_part)

    own = ta_sum(own)
    own_left = shifted(own[chans - 2 * STRIDE :, chans - 2 * STRIDE :], "ch", 1)
    own_right = shifted(own[:STRIDE, :STRIDE], "ch", -1)
    own, lowers, uppers = lax.optimization_barrier((own, lowers, uppers))

    for number in range(chunks):
        lower_part, gauged, upper_part = lowers[number], gaugeds[number], uppers[number]
        left = gram(lower_part, gauged)
        tail = jnp.concatenate([lower_part[STRIDE:], gauged], axis=0)
        right = gram(tail, upper_part)
        cross_left = left if cross_left is None else cross_left + left
        cross_right = right if cross_right is None else cross_right + right

    packed = ta_sum(jnp.concatenate([cross_left[:, :STRIDE], cross_left[:, STRIDE:], cross_right], axis=0))
    tiles_left = 2 * STRIDE
    cross_left = jnp.concatenate(
        [packed[:tiles_left], packed[tiles_left : 2 * tiles_left]], axis=1
    )
    cross_right = packed[2 * tiles_left :]

    zeros = jnp.zeros((STRIDE, STRIDE), jnp.float32)
    top = jnp.concatenate(
        [own_left, cross_left, jnp.concatenate([zeros, cross_right[:STRIDE]], axis=0)], axis=1
    )
    middle = jnp.concatenate(
        [cross_left.T, own, cross_right[STRIDE:]], axis=1
    )
    corner = jnp.concatenate([zeros, cross_right[:STRIDE].T], axis=1)
    bottom = jnp.concatenate([corner, cross_right[STRIDE:].T, own_right], axis=1)
    band = jnp.concatenate([top, middle, bottom], axis=0) / total_time

    rounded = subspace(band, start_basis.T, windows)
    cleaned = None
    for number in range(chunks):
        cleaned = clean(
            lowers[number], gaugeds[number], uppers[number], rounded, samples, number * piece, cleaned
        )
    return cleaned


def solution(mesh):
    return jax.shard_map(
        per_device,
        mesh=mesh,
        in_specs=(P("ch", "ta"), P(), P()),
        out_specs=P("ch", "ta"),
        check_vma=False,
    )
```

```python
import math

import jax
import jax.numpy as jnp
from jax import lax
from jax.experimental import pallas as pl
from jax.experimental.pallas import tpu as pltpu
from jax.sharding import PartitionSpec as P

TAPS = 129
GAUGE = 4
STRIDE = 128
RANK = 16
ITERS = 6
WIN = 512


def with_halo(block, sides, width):
    for axis, dim in sides:
        count = lax.axis_size(axis)
        forward = [(i, i + 1) for i in range(count - 1)]
        backward = [(target, source) for source, target in forward]
        low = lax.ppermute(
            lax.slice_in_dim(block, block.shape[dim] - width, None, axis=dim), axis, forward
        )
        high = lax.ppermute(lax.slice_in_dim(block, 0, width, axis=dim), axis, backward)
        block = jnp.concatenate([low, block, high], axis=dim)
    return block


def shifted(value, axis, steps):
    count = lax.axis_size(axis)
    first, last = (max(0, -steps), min(count, count - steps))
    return lax.ppermute(value, axis, [(source, source + steps) for source in range(first, last)])


def toeplitz_band(taps, width):
    count = taps.shape[0]
    line = jnp.concatenate([taps, jnp.zeros((width,), taps.dtype)])
    flat = jnp.tile(line, width)[: width * (count + width - 1)]
    return flat.reshape(width, count + width - 1).T


def gram(a, b):
    return lax.dot_general(a, b, (((1,), (1,)), ((), ())), preferred_element_type=jnp.float32)


def orthonormal_rows(image, rows, lanes):
    rank = image.shape[0]
    gram_mat = lax.dot_general(
        image, image, (((1,), (1,)), ((), ())), precision=lax.Precision.HIGHEST,
        preferred_element_type=jnp.float32,
    )
    result = image
    for j in range(rank):
        column = jnp.sum(jnp.where(lanes == j, gram_mat, 0.0), axis=1, keepdims=True)
        scale = 1.0 / jnp.sqrt(column[j : j + 1, :])
        factor = column * scale
        pivot_row = gram_mat[j : j + 1, :] * scale
        image_row = result[j : j + 1, :] * scale
        below = rows > j
        gram_mat = jnp.where(below, gram_mat - factor * pivot_row, gram_mat)
        result = jnp.where(below, result - factor * image_row, jnp.where(rows == j, image_row, result))
    return result


def subspace_kernel(band_ref, start_ref, out_ref):
    windows = out_ref.shape[0]
    rank, win = start_ref.shape
    rows = lax.broadcasted_iota(jnp.int32, (rank, 1), 0)
    lanes = lax.broadcasted_iota(jnp.int32, (rank, rank), 1)
    bases = [start_ref[...] for _ in range(windows)]
    for sweep in range(ITERS):
        for number in range(windows):
            lo = number * STRIDE
            scatter_mat = band_ref[lo : lo + win, lo : lo + win]
            image = jnp.dot(
                bases[number], scatter_mat, precision=lax.Precision.HIGHEST,
                preferred_element_type=jnp.float32,
            )
            bases[number] = orthonormal_rows(image, rows, lanes)
    for number in range(windows):
        out_ref[number] = bases[number].astype(out_ref.dtype)


def subspace(band, start_t, windows):
    return pl.pallas_call(
        subspace_kernel,
        out_shape=jax.ShapeDtypeStruct((windows,) + start_t.shape, jnp.bfloat16),
        in_specs=[
            pl.BlockSpec(memory_space=pltpu.VMEM),
            pl.BlockSpec(memory_space=pltpu.VMEM),
        ],
        out_specs=pl.BlockSpec(memory_space=pltpu.VMEM),
    )(band, start_t)


def fir_kernel(left_ref, right_ref, prev_ref, cur_ref, next_ref, lo_ref, mid_ref, hi_ref, out_ref, *, first, last):
    block = (pl.program_id(0) + first) % (last + 1)
    before = jnp.where(block == 0, left_ref[...], prev_ref[...])
    after = jnp.where(block == last, right_ref[...], next_ref[...])
    out_ref[...] = (
        jnp.dot(before, lo_ref[...], preferred_element_type=jnp.float32)
        + jnp.dot(cur_ref[...], mid_ref[...], preferred_element_type=jnp.float32)
        + jnp.dot(after, hi_ref[...], preferred_element_type=jnp.float32)
    )


def fir(raw, left, right, band, start, length):
    chans, samples = raw.shape
    width = band.shape[1]
    edge = 128
    step = width // edge
    first = start // width
    blocks = samples // width
    lo, mid, hi = band[:edge], band[edge : edge + width], band[edge + width :]
    kernel = lambda *refs: fir_kernel(*refs, first=first, last=blocks - 1)
    full = lambda b: (0, 0)
    at = lambda b: (b + first) % blocks
    return pl.pallas_call(
        kernel,
        grid=(length // width,),
        out_shape=jax.ShapeDtypeStruct((chans, length), jnp.float32),
        in_specs=[
            pl.BlockSpec((chans, edge), full),
            pl.BlockSpec((chans, edge), full),
            pl.BlockSpec((chans, edge), lambda b: (0, jnp.maximum(at(b) * step - 1, 0))),
            pl.BlockSpec((chans, width), lambda b: (0, at(b))),
            pl.BlockSpec((chans, edge), lambda b: (0, jnp.minimum((at(b) + 1) * step, samples // edge - 1))),
            pl.BlockSpec((edge, width), full),
            pl.BlockSpec((width, width), full),
            pl.BlockSpec((edge, width), full),
        ],
        out_specs=pl.BlockSpec((chans, width), lambda b: (0, b)),
    )(left, right, raw, raw, raw, lo, mid, hi)


def clean_kernel(lower_ref, own_ref, upper_ref, basis_ref, middle_ref, *rest):
    out_ref = rest[-1]
    tiles = own_ref.shape[0] // STRIDE
    parts = [lower_ref[k * STRIDE : (k + 1) * STRIDE] for k in range(2)]
    parts += [own_ref[k * STRIDE : (k + 1) * STRIDE] for k in range(tiles)]
    parts.append(upper_ref[...])
    for number in range(tiles):
        coeffs = jnp.dot(basis_ref[number, :, 0:STRIDE], parts[number], preferred_element_type=jnp.float32)
        for k in range(1, WIN // STRIDE):
            coeffs = coeffs + jnp.dot(
                basis_ref[number, :, k * STRIDE : (k + 1) * STRIDE], parts[number + k],
                preferred_element_type=jnp.float32,
            )
        fitted = jnp.dot(
            middle_ref[number], coeffs.astype(jnp.bfloat16), preferred_element_type=jnp.float32
        )
        out_ref[number * STRIDE : (number + 1) * STRIDE] = (
            parts[number + 2].astype(jnp.float32) - fitted
        ).astype(out_ref.dtype)


def clean(lower, own, upper, rounded, total, start, into):
    chans, samples = own.shape
    width = math.gcd(math.gcd(samples, start) if start else samples, 512)
    first = start // width
    middle = jnp.swapaxes(rounded[:, :, 2 * STRIDE : 3 * STRIDE], 1, 2)
    return pl.pallas_call(
        clean_kernel,
        grid=(samples // width,),
        out_shape=jax.ShapeDtypeStruct((chans, total), own.dtype),
        in_specs=[
            pl.BlockSpec((lower.shape[0], width), lambda b: (0, b)),
            pl.BlockSpec((chans, width), lambda b: (0, b)),
            pl.BlockSpec((STRIDE, width), lambda b: (0, b)),
            pl.BlockSpec(rounded.shape, lambda b: (0, 0, 0)),
            pl.BlockSpec(middle.shape, lambda b: (0, 0, 0)),
        ] + ([] if into is None else [pl.BlockSpec(memory_space=pl.ANY)]),
        out_specs=pl.BlockSpec((chans, width), lambda b: (0, (b + first) % (total // width))),
        input_output_aliases={} if into is None else {5: 0},
    )(lower, own, upper, rounded, middle, *([] if into is None else [into]))


def ta_sum(value):
    count = lax.axis_size("ta")
    if count != 4:
        return lax.psum(value, "ta")
    core = lax.axis_index("ta") % 2
    rows = value.shape[0] // 2
    low, high = value[:rows], value[rows:]
    mine = jnp.where(core == 0, low, high)
    theirs = jnp.where(core == 0, high, low)
    partner = [(i, i ^ 1) for i in range(count)]
    across = [(i, i ^ 2) for i in range(count)]
    part = mine + lax.ppermute(theirs, "ta", partner)
    part = part + lax.ppermute(part, "ta", across)
    other = lax.ppermute(part, "ta", partner)
    return jnp.where(core == 0, jnp.concatenate([part, other]), jnp.concatenate([other, part]))


def per_device(raw, fir_taps, start_basis):
    chans = raw.shape[0]
    samples = raw.shape[1]
    half = (TAPS - 1) // 2
    count = lax.axis_size("ta")
    forward = [(i, i + 1) for i in range(count - 1)]
    backward = [(target, source) for source, target in forward]
    blank = jnp.zeros((chans, STRIDE - half), raw.dtype)
    left = jnp.concatenate([blank, lax.ppermute(raw[:, samples - half :], "ta", forward)], axis=1)
    right = jnp.concatenate([lax.ppermute(raw[:, :half], "ta", backward), blank], axis=1)
    width = math.gcd(samples, 512)
    band = jnp.pad(toeplitz_band(fir_taps, width), ((half, half), (0, 0)))
    source = raw
    chunks = 2 if samples % 1024 == 0 else 1
    piece = samples // chunks
    tiles = chans // STRIDE
    windows = tiles
    total_time = samples * lax.axis_size("ta")
    gaugeds, lowers, uppers = [], [], []
    own = cross_left = cross_right = None
    for number in range(chunks):
        start = number * piece + width
        edges = (left, right) if number == chunks - 1 else (source[:, :STRIDE], source[:, :STRIDE])
        filtered = fir(source, *edges, band, start, piece)
        extended = with_halo(filtered, (("ch", 0),), GAUGE)
        gauged = (extended[2 * GAUGE :] - extended[: -2 * GAUGE]).astype(jnp.bfloat16)
        lower_part = shifted(gauged[chans - 2 * STRIDE :], "ch", 1)
        upper_part = shifted(gauged[:STRIDE], "ch", -1)
        local = gram(gauged, gauged)
        own = local if own is None else own + local
        gaugeds.append(gauged)
        source, gauged = lax.optimization_barrier((source, gauged))
        lowers.append(lower_part)
        uppers.append(upper_part)

    own = ta_sum(own)
    own_left = shifted(own[chans - 2 * STRIDE :, chans - 2 * STRIDE :], "ch", 1)
    own_right = shifted(own[:STRIDE, :STRIDE], "ch", -1)
    own, lowers, uppers = lax.optimization_barrier((own, lowers, uppers))

    for number in range(chunks):
        lower_part, gauged, upper_part = lowers[number], gaugeds[number], uppers[number]
        left = gram(lower_part, gauged)
        tail = jnp.concatenate([lower_part[STRIDE:], gauged], axis=0)
        right = gram(tail, upper_part)
        cross_left = left if cross_left is None else cross_left + left
        cross_right = right if cross_right is None else cross_right + right

    packed = ta_sum(jnp.concatenate([cross_left[:, :STRIDE], cross_left[:, STRIDE:], cross_right], axis=0))
    tiles_left = 2 * STRIDE
    cross_left = jnp.concatenate(
        [packed[:tiles_left], packed[tiles_left : 2 * tiles_left]], axis=1
    )
    cross_right = packed[2 * tiles_left :]

    zeros = jnp.zeros((STRIDE, STRIDE), jnp.float32)
    top = jnp.concatenate(
        [own_left, cross_left, jnp.concatenate([zeros, cross_right[:STRIDE]], axis=0)], axis=1
    )
    middle = jnp.concatenate(
        [cross_left.T, own, cross_right[STRIDE:]], axis=1
    )
    corner = jnp.concatenate([zeros, cross_right[:STRIDE].T], axis=1)
    bottom = jnp.concatenate([corner, cross_right[STRIDE:].T, own_right], axis=1)
    band = jnp.concatenate([top, middle, bottom], axis=0) / total_time

    rounded = subspace(band, start_basis.T, windows)
    cleaned = None
    for number in range(chunks):
        cleaned = clean(
            lowers[number], gaugeds[number], uppers[number], rounded, samples, number * piece + width, cleaned
        )
    return cleaned


def solution(mesh):
    return jax.shard_map(
        per_device,
        mesh=mesh,
        in_specs=(P("ch", "ta"), P(), P()),
        out_specs=P("ch", "ta"),
        check_vma=False,
    )
```

```python
import math

import jax
import jax.numpy as jnp
from jax import lax
from jax.experimental import pallas as pl
from jax.experimental.pallas import tpu as pltpu
from jax.sharding import PartitionSpec as P

TAPS = 129
GAUGE = 4
STRIDE = 128
RANK = 16
ITERS = 6
WIN = 512


def with_halo(block, sides, width):
    for axis, dim in sides:
        count = lax.axis_size(axis)
        forward = [(i, i + 1) for i in range(count - 1)]
        backward = [(target, source) for source, target in forward]
        low = lax.ppermute(
            lax.slice_in_dim(block, block.shape[dim] - width, None, axis=dim), axis, forward
        )
        high = lax.ppermute(lax.slice_in_dim(block, 0, width, axis=dim), axis, backward)
        block = jnp.concatenate([low, block, high], axis=dim)
    return block


def shifted(value, axis, steps):
    count = lax.axis_size(axis)
    first, last = (max(0, -steps), min(count, count - steps))
    return lax.ppermute(value, axis, [(source, source + steps) for source in range(first, last)])


def toeplitz_band(taps, width):
    count = taps.shape[0]
    line = jnp.concatenate([taps, jnp.zeros((width,), taps.dtype)])
    flat = jnp.tile(line, width)[: width * (count + width - 1)]
    return flat.reshape(width, count + width - 1).T


def gram(a, b):
    return lax.dot_general(a, b, (((1,), (1,)), ((), ())), preferred_element_type=jnp.float32)


def orthonormal_rows(image, rows, lanes):
    rank = image.shape[0]
    gram_mat = lax.dot_general(
        image, image, (((1,), (1,)), ((), ())), precision=lax.Precision.HIGHEST,
        preferred_element_type=jnp.float32,
    )
    result = image
    for j in range(rank):
        column = jnp.sum(jnp.where(lanes == j, gram_mat, 0.0), axis=1, keepdims=True)
        scale = 1.0 / jnp.sqrt(column[j : j + 1, :])
        factor = column * scale
        pivot_row = gram_mat[j : j + 1, :] * scale
        image_row = result[j : j + 1, :] * scale
        below = rows > j
        gram_mat = jnp.where(below, gram_mat - factor * pivot_row, gram_mat)
        result = jnp.where(below, result - factor * image_row, jnp.where(rows == j, image_row, result))
    return result


def subspace_kernel(band_ref, start_ref, out_ref):
    windows = out_ref.shape[0]
    rank, win = start_ref.shape
    rows = lax.broadcasted_iota(jnp.int32, (rank, 1), 0)
    lanes = lax.broadcasted_iota(jnp.int32, (rank, rank), 1)
    bases = [start_ref[...] for _ in range(windows)]
    for sweep in range(ITERS):
        for number in range(windows):
            lo = number * STRIDE
            scatter_mat = band_ref[lo : lo + win, lo : lo + win]
            image = jnp.dot(
                bases[number], scatter_mat, precision=lax.Precision.HIGHEST,
                preferred_element_type=jnp.float32,
            )
            bases[number] = orthonormal_rows(image, rows, lanes)
    for number in range(windows):
        out_ref[number] = bases[number].astype(out_ref.dtype)


def subspace(band, start_t, windows):
    return pl.pallas_call(
        subspace_kernel,
        out_shape=jax.ShapeDtypeStruct((windows,) + start_t.shape, jnp.bfloat16),
        in_specs=[
            pl.BlockSpec(memory_space=pltpu.VMEM),
            pl.BlockSpec(memory_space=pltpu.VMEM),
        ],
        out_specs=pl.BlockSpec(memory_space=pltpu.VMEM),
    )(band, start_t)


def fir_kernel(left_ref, right_ref, prev_ref, cur_ref, next_ref, lo_ref, mid_ref, hi_ref, out_ref, *, first, last):
    block = (pl.program_id(0) + first) % (last + 1)
    before = jnp.where(block == 0, left_ref[...], prev_ref[...])
    after = jnp.where(block == last, right_ref[...], next_ref[...])
    out_ref[...] = (
        jnp.dot(before, lo_ref[...], preferred_element_type=jnp.float32)
        + jnp.dot(cur_ref[...], mid_ref[...], preferred_element_type=jnp.float32)
        + jnp.dot(after, hi_ref[...], preferred_element_type=jnp.float32)
    )


def fir(raw, left, right, band, start, length):
    chans, samples = raw.shape
    width = band.shape[1]
    edge = 128
    step = width // edge
    first = start // width
    blocks = samples // width
    lo, mid, hi = band[:edge], band[edge : edge + width], band[edge + width :]
    kernel = lambda *refs: fir_kernel(*refs, first=first, last=blocks - 1)
    full = lambda b: (0, 0)
    at = lambda b: (b + first) % blocks
    return pl.pallas_call(
        kernel,
        grid=(length // width,),
        out_shape=jax.ShapeDtypeStruct((chans, length), jnp.float32),
        in_specs=[
            pl.BlockSpec((chans, edge), full),
            pl.BlockSpec((chans, edge), full),
            pl.BlockSpec((chans, edge), lambda b: (0, jnp.maximum(at(b) * step - 1, 0))),
            pl.BlockSpec((chans, width), lambda b: (0, at(b))),
            pl.BlockSpec((chans, edge), lambda b: (0, jnp.minimum((at(b) + 1) * step, samples // edge - 1))),
            pl.BlockSpec((edge, width), full),
            pl.BlockSpec((width, width), full),
            pl.BlockSpec((edge, width), full),
        ],
        out_specs=pl.BlockSpec((chans, width), lambda b: (0, b)),
    )(left, right, raw, raw, raw, lo, mid, hi)


def clean_kernel(lower_ref, own_ref, upper_ref, basis_ref, middle_ref, *rest):
    out_ref = rest[-1]
    tiles = own_ref.shape[0] // STRIDE
    parts = [lower_ref[k * STRIDE : (k + 1) * STRIDE] for k in range(2)]
    parts += [own_ref[k * STRIDE : (k + 1) * STRIDE] for k in range(tiles)]
    parts.append(upper_ref[...])
    for number in range(tiles):
        coeffs = jnp.dot(basis_ref[number, :, 0:STRIDE], parts[number], preferred_element_type=jnp.float32)
        for k in range(1, WIN // STRIDE):
            coeffs = coeffs + jnp.dot(
                basis_ref[number, :, k * STRIDE : (k + 1) * STRIDE], parts[number + k],
                preferred_element_type=jnp.float32,
            )
        fitted = jnp.dot(
            middle_ref[number], coeffs.astype(jnp.bfloat16), preferred_element_type=jnp.float32
        )
        out_ref[number * STRIDE : (number + 1) * STRIDE] = (
            parts[number + 2].astype(jnp.float32) - fitted
        ).astype(out_ref.dtype)


def clean(lower, own, upper, rounded, total, start, into):
    chans, samples = own.shape
    width = math.gcd(math.gcd(samples, start) if start else samples, 512)
    first = start // width
    middle = jnp.swapaxes(rounded[:, :, 2 * STRIDE : 3 * STRIDE], 1, 2)
    return pl.pallas_call(
        clean_kernel,
        grid=(samples // width,),
        out_shape=jax.ShapeDtypeStruct((chans, total), own.dtype),
        in_specs=[
            pl.BlockSpec((lower.shape[0], width), lambda b: (0, b)),
            pl.BlockSpec((chans, width), lambda b: (0, b)),
            pl.BlockSpec((STRIDE, width), lambda b: (0, b)),
            pl.BlockSpec(rounded.shape, lambda b: (0, 0, 0)),
            pl.BlockSpec(middle.shape, lambda b: (0, 0, 0)),
        ] + ([] if into is None else [pl.BlockSpec(memory_space=pl.ANY)]),
        out_specs=pl.BlockSpec((chans, width), lambda b: (0, (b + first) % (total // width))),
        input_output_aliases={} if into is None else {5: 0},
    )(lower, own, upper, rounded, middle, *([] if into is None else [into]))


def ta_sum(value):
    count = lax.axis_size("ta")
    if count != 4:
        return lax.psum(value, "ta")
    core = lax.axis_index("ta") % 2
    rows = value.shape[0] // 2
    low, high = value[:rows], value[rows:]
    mine = jnp.where(core == 0, low, high)
    theirs = jnp.where(core == 0, high, low)
    partner = [(i, i ^ 1) for i in range(count)]
    across = [(i, i ^ 2) for i in range(count)]
    part = mine + lax.ppermute(theirs, "ta", partner)
    part = part + lax.ppermute(part, "ta", across)
    other = lax.ppermute(part, "ta", partner)
    return jnp.where(core == 0, jnp.concatenate([part, other]), jnp.concatenate([other, part]))


def per_device(raw, fir_taps, start_basis):
    chans = raw.shape[0]
    samples = raw.shape[1]
    half = (TAPS - 1) // 2
    count = lax.axis_size("ta")
    forward = [(i, i + 1) for i in range(count - 1)]
    backward = [(target, source) for source, target in forward]
    blank = jnp.zeros((chans, STRIDE - half), raw.dtype)
    left = jnp.concatenate([blank, lax.ppermute(raw[:, samples - half :], "ta", forward)], axis=1)
    right = jnp.concatenate([lax.ppermute(raw[:, :half], "ta", backward), blank], axis=1)
    width = math.gcd(samples, 512)
    band = jnp.pad(toeplitz_band(fir_taps, width), ((half, half), (0, 0)))
    chunks = 2 if samples % 1024 == 0 else 1
    piece = samples // chunks
    tiles = chans // STRIDE
    windows = tiles
    total_time = samples * lax.axis_size("ta")
    gaugeds, lowers, uppers = [], [], []
    own = cross_left = cross_right = None
    filters = []
    for number in range(chunks):
        start = number * piece + width
        edges = (left, right) if number == chunks - 1 else (raw[:, :STRIDE], raw[:, :STRIDE])
        filters.append(fir(raw, *edges, band, start, piece))
    filters = lax.optimization_barrier(filters)
    for number in range(chunks):
        extended = with_halo(filters[number], (("ch", 0),), GAUGE)
        gauged = (extended[2 * GAUGE :] - extended[: -2 * GAUGE]).astype(jnp.bfloat16)
        lower_part = shifted(gauged[chans - 2 * STRIDE :], "ch", 1)
        upper_part = shifted(gauged[:STRIDE], "ch", -1)
        local = gram(gauged, gauged)
        own = local if own is None else own + local
        gaugeds.append(gauged)
        lowers.append(lower_part)
        uppers.append(upper_part)

    own = ta_sum(own)
    own_left = shifted(own[chans - 2 * STRIDE :, chans - 2 * STRIDE :], "ch", 1)
    own_right = shifted(own[:STRIDE, :STRIDE], "ch", -1)
    own, lowers, uppers = lax.optimization_barrier((own, lowers, uppers))

    for number in range(chunks):
        lower_part, gauged, upper_part = lowers[number], gaugeds[number], uppers[number]
        left = gram(lower_part, gauged)
        tail = jnp.concatenate([lower_part[STRIDE:], gauged], axis=0)
        right = gram(tail, upper_part)
        cross_left = left if cross_left is None else cross_left + left
        cross_right = right if cross_right is None else cross_right + right

    packed = ta_sum(jnp.concatenate([cross_left[:, :STRIDE], cross_left[:, STRIDE:], cross_right], axis=0))
    tiles_left = 2 * STRIDE
    cross_left = jnp.concatenate(
        [packed[:tiles_left], packed[tiles_left : 2 * tiles_left]], axis=1
    )
    cross_right = packed[2 * tiles_left :]

    zeros = jnp.zeros((STRIDE, STRIDE), jnp.float32)
    top = jnp.concatenate(
        [own_left, cross_left, jnp.concatenate([zeros, cross_right[:STRIDE]], axis=0)], axis=1
    )
    middle = jnp.concatenate(
        [cross_left.T, own, cross_right[STRIDE:]], axis=1
    )
    corner = jnp.concatenate([zeros, cross_right[:STRIDE].T], axis=1)
    bottom = jnp.concatenate([corner, cross_right[STRIDE:].T, own_right], axis=1)
    band = jnp.concatenate([top, middle, bottom], axis=0) / total_time

    rounded = subspace(band, start_basis.T, windows)
    cleaned = None
    for number in range(chunks):
        cleaned = clean(
            lowers[number], gaugeds[number], uppers[number], rounded, samples, number * piece + width, cleaned
        )
    return cleaned


def solution(mesh):
    return jax.shard_map(
        per_device,
        mesh=mesh,
        in_specs=(P("ch", "ta"), P(), P()),
        out_specs=P("ch", "ta"),
        check_vma=False,
    )
```

```python
import math

import jax
import jax.numpy as jnp
from jax import lax
from jax.experimental import pallas as pl
from jax.experimental.pallas import tpu as pltpu
from jax.sharding import PartitionSpec as P

TAPS = 129
GAUGE = 4
STRIDE = 128
RANK = 16
ITERS = 6
WIN = 512


def with_halo(block, sides, width):
    for axis, dim in sides:
        count = lax.axis_size(axis)
        forward = [(i, i + 1) for i in range(count - 1)]
        backward = [(target, source) for source, target in forward]
        low = lax.ppermute(
            lax.slice_in_dim(block, block.shape[dim] - width, None, axis=dim), axis, forward
        )
        high = lax.ppermute(lax.slice_in_dim(block, 0, width, axis=dim), axis, backward)
        block = jnp.concatenate([low, block, high], axis=dim)
    return block


def shifted(value, axis, steps):
    count = lax.axis_size(axis)
    first, last = (max(0, -steps), min(count, count - steps))
    return lax.ppermute(value, axis, [(source, source + steps) for source in range(first, last)])


def toeplitz_band(taps, width):
    count = taps.shape[0]
    line = jnp.concatenate([taps, jnp.zeros((width,), taps.dtype)])
    flat = jnp.tile(line, width)[: width * (count + width - 1)]
    return flat.reshape(width, count + width - 1).T


def gram(a, b):
    return lax.dot_general(a, b, (((1,), (1,)), ((), ())), preferred_element_type=jnp.float32)


def orthonormal_rows(image, rows, lanes):
    rank = image.shape[0]
    gram_mat = lax.dot_general(
        image, image, (((1,), (1,)), ((), ())), precision=lax.Precision.HIGHEST,
        preferred_element_type=jnp.float32,
    )
    result = image
    for j in range(rank):
        column = jnp.sum(jnp.where(lanes == j, gram_mat, 0.0), axis=1, keepdims=True)
        scale = 1.0 / jnp.sqrt(column[j : j + 1, :])
        factor = column * scale
        pivot_row = gram_mat[j : j + 1, :] * scale
        image_row = result[j : j + 1, :] * scale
        below = rows > j
        gram_mat = jnp.where(below, gram_mat - factor * pivot_row, gram_mat)
        result = jnp.where(below, result - factor * image_row, jnp.where(rows == j, image_row, result))
    return result


def subspace_kernel(band_ref, start_ref, out_ref):
    windows = out_ref.shape[0]
    rank, win = start_ref.shape
    rows = lax.broadcasted_iota(jnp.int32, (rank, 1), 0)
    lanes = lax.broadcasted_iota(jnp.int32, (rank, rank), 1)
    bases = [start_ref[...] for _ in range(windows)]
    for sweep in range(ITERS):
        for number in range(windows):
            lo = number * STRIDE
            scatter_mat = band_ref[lo : lo + win, lo : lo + win]
            image = jnp.dot(
                bases[number], scatter_mat, precision=lax.Precision.HIGHEST,
                preferred_element_type=jnp.float32,
            )
            bases[number] = orthonormal_rows(image, rows, lanes)
    for number in range(windows):
        out_ref[number] = bases[number].astype(out_ref.dtype)


def subspace(band, start_t, windows):
    return pl.pallas_call(
        subspace_kernel,
        out_shape=jax.ShapeDtypeStruct((windows,) + start_t.shape, jnp.bfloat16),
        in_specs=[
            pl.BlockSpec(memory_space=pltpu.VMEM),
            pl.BlockSpec(memory_space=pltpu.VMEM),
        ],
        out_specs=pl.BlockSpec(memory_space=pltpu.VMEM),
    )(band, start_t)


def fir_kernel(left_ref, right_ref, prev_ref, cur_ref, next_ref, lo_ref, mid_ref, hi_ref, out_ref, *, first, last):
    block = (pl.program_id(0) + first) % (last + 1)
    before = jnp.where(block == 0, left_ref[...], prev_ref[...])
    after = jnp.where(block == last, right_ref[...], next_ref[...])
    out_ref[...] = (
        jnp.dot(before, lo_ref[...], preferred_element_type=jnp.float32)
        + jnp.dot(cur_ref[...], mid_ref[...], preferred_element_type=jnp.float32)
        + jnp.dot(after, hi_ref[...], preferred_element_type=jnp.float32)
    )


def fir(raw, left, right, band, start, length):
    chans, samples = raw.shape
    width = band.shape[1]
    edge = 128
    step = width // edge
    first = start // width
    blocks = samples // width
    lo, mid, hi = band[:edge], band[edge : edge + width], band[edge + width :]
    kernel = lambda *refs: fir_kernel(*refs, first=first, last=blocks - 1)
    full = lambda b: (0, 0)
    at = lambda b: (b + first) % blocks
    return pl.pallas_call(
        kernel,
        grid=(length // width,),
        out_shape=jax.ShapeDtypeStruct((chans, length), jnp.float32),
        in_specs=[
            pl.BlockSpec((chans, edge), full),
            pl.BlockSpec((chans, edge), full),
            pl.BlockSpec((chans, edge), lambda b: (0, jnp.maximum(at(b) * step - 1, 0))),
            pl.BlockSpec((chans, width), lambda b: (0, at(b))),
            pl.BlockSpec((chans, edge), lambda b: (0, jnp.minimum((at(b) + 1) * step, samples // edge - 1))),
            pl.BlockSpec((edge, width), full),
            pl.BlockSpec((width, width), full),
            pl.BlockSpec((edge, width), full),
        ],
        out_specs=pl.BlockSpec((chans, width), lambda b: (0, b)),
    )(left, right, raw, raw, raw, lo, mid, hi)


def clean_kernel(lower_ref, own_ref, upper_ref, basis_ref, middle_ref, *rest):
    out_ref = rest[-1]
    tiles = own_ref.shape[0] // STRIDE
    parts = [lower_ref[k * STRIDE : (k + 1) * STRIDE] for k in range(2)]
    parts += [own_ref[k * STRIDE : (k + 1) * STRIDE] for k in range(tiles)]
    parts.append(upper_ref[...])
    for number in range(tiles):
        coeffs = jnp.dot(basis_ref[number, :, 0:STRIDE], parts[number], preferred_element_type=jnp.float32)
        for k in range(1, WIN // STRIDE):
            coeffs = coeffs + jnp.dot(
                basis_ref[number, :, k * STRIDE : (k + 1) * STRIDE], parts[number + k],
                preferred_element_type=jnp.float32,
            )
        fitted = jnp.dot(
            middle_ref[number], coeffs.astype(jnp.bfloat16), preferred_element_type=jnp.float32
        )
        out_ref[number * STRIDE : (number + 1) * STRIDE] = (
            parts[number + 2].astype(jnp.float32) - fitted
        ).astype(out_ref.dtype)


def clean(lower, own, upper, rounded, total, start, into):
    chans, samples = own.shape
    width = math.gcd(math.gcd(samples, start) if start else samples, 512)
    first = start // width
    middle = jnp.swapaxes(rounded[:, :, 2 * STRIDE : 3 * STRIDE], 1, 2)
    return pl.pallas_call(
        clean_kernel,
        grid=(samples // width,),
        out_shape=jax.ShapeDtypeStruct((chans, total), own.dtype),
        in_specs=[
            pl.BlockSpec((lower.shape[0], width), lambda b: (0, b)),
            pl.BlockSpec((chans, width), lambda b: (0, b)),
            pl.BlockSpec((STRIDE, width), lambda b: (0, b)),
            pl.BlockSpec(rounded.shape, lambda b: (0, 0, 0)),
            pl.BlockSpec(middle.shape, lambda b: (0, 0, 0)),
        ] + ([] if into is None else [pl.BlockSpec(memory_space=pl.ANY)]),
        out_specs=pl.BlockSpec((chans, width), lambda b: (0, (b + first) % (total // width))),
        input_output_aliases={} if into is None else {5: 0},
    )(lower, own, upper, rounded, middle, *([] if into is None else [into]))


def ta_sum(value):
    count = lax.axis_size("ta")
    if count != 4:
        return lax.psum(value, "ta")
    core = lax.axis_index("ta") % 2
    rows = value.shape[0] // 2
    low, high = value[:rows], value[rows:]
    mine = jnp.where(core == 0, low, high)
    theirs = jnp.where(core == 0, high, low)
    partner = [(i, i ^ 1) for i in range(count)]
    across = [(i, i ^ 2) for i in range(count)]
    part = mine + lax.ppermute(theirs, "ta", partner)
    part = part + lax.ppermute(part, "ta", across)
    other = lax.ppermute(part, "ta", partner)
    return jnp.where(core == 0, jnp.concatenate([part, other]), jnp.concatenate([other, part]))


def ta_sum_full(value):
    count = lax.axis_size("ta")
    if count != 4:
        return lax.psum(value, "ta")
    value = value + lax.ppermute(value, "ta", [(i, i ^ 1) for i in range(count)])
    return value + lax.ppermute(value, "ta", [(i, i ^ 2) for i in range(count)])


def per_device(raw, fir_taps, start_basis):
    chans = raw.shape[0]
    samples = raw.shape[1]
    half = (TAPS - 1) // 2
    count = lax.axis_size("ta")
    forward = [(i, i + 1) for i in range(count - 1)]
    backward = [(target, source) for source, target in forward]
    blank = jnp.zeros((chans, STRIDE - half), raw.dtype)
    left = jnp.concatenate([blank, lax.ppermute(raw[:, samples - half :], "ta", forward)], axis=1)
    right = jnp.concatenate([lax.ppermute(raw[:, :half], "ta", backward), blank], axis=1)
    width = math.gcd(samples, 512)
    band = jnp.pad(toeplitz_band(fir_taps, width), ((half, half), (0, 0)))
    chunks = 2 if samples % 1024 == 0 else 1
    piece = samples // chunks
    tiles = chans // STRIDE
    windows = tiles
    total_time = samples * lax.axis_size("ta")
    gaugeds, lowers, uppers = [], [], []
    own = cross_left = cross_right = None
    filters = []
    for number in range(chunks):
        start = number * piece + width
        edges = (left, right) if number == chunks - 1 else (raw[:, :STRIDE], raw[:, :STRIDE])
        filters.append(fir(raw, *edges, band, start, piece))
    filters = lax.optimization_barrier(filters)
    for number in range(chunks):
        extended = with_halo(filters[number], (("ch", 0),), GAUGE)
        gauged = (extended[2 * GAUGE :] - extended[: -2 * GAUGE]).astype(jnp.bfloat16)
        lower_part = shifted(gauged[chans - 2 * STRIDE :], "ch", 1)
        upper_part = shifted(gauged[:STRIDE], "ch", -1)
        local = gram(gauged, gauged)
        own = local if own is None else own + local
        gaugeds.append(gauged)
        lowers.append(lower_part)
        uppers.append(upper_part)

    own = ta_sum(own)
    own_left = shifted(own[chans - 2 * STRIDE :, chans - 2 * STRIDE :], "ch", 1)
    own_right = shifted(own[:STRIDE, :STRIDE], "ch", -1)
    own, lowers, uppers = lax.optimization_barrier((own, lowers, uppers))

    for number in range(chunks):
        lower_part, gauged, upper_part = lowers[number], gaugeds[number], uppers[number]
        left = gram(lower_part, gauged)
        tail = jnp.concatenate([lower_part[STRIDE:], gauged], axis=0)
        right = gram(tail, upper_part)
        cross_left = left if cross_left is None else cross_left + left
        cross_right = right if cross_right is None else cross_right + right

    packed = ta_sum_full(jnp.concatenate([cross_left[:, :STRIDE], cross_left[:, STRIDE:], cross_right], axis=0))
    tiles_left = 2 * STRIDE
    cross_left = jnp.concatenate(
        [packed[:tiles_left], packed[tiles_left : 2 * tiles_left]], axis=1
    )
    cross_right = packed[2 * tiles_left :]

    zeros = jnp.zeros((STRIDE, STRIDE), jnp.float32)
    top = jnp.concatenate(
        [own_left, cross_left, jnp.concatenate([zeros, cross_right[:STRIDE]], axis=0)], axis=1
    )
    middle = jnp.concatenate(
        [cross_left.T, own, cross_right[STRIDE:]], axis=1
    )
    corner = jnp.concatenate([zeros, cross_right[:STRIDE].T], axis=1)
    bottom = jnp.concatenate([corner, cross_right[STRIDE:].T, own_right], axis=1)
    band = jnp.concatenate([top, middle, bottom], axis=0) / total_time

    rounded = subspace(band, start_basis.T, windows)
    cleaned = None
    for number in range(chunks):
        cleaned = clean(
            lowers[number], gaugeds[number], uppers[number], rounded, samples, number * piece + width, cleaned
        )
    return cleaned


def solution(mesh):
    return jax.shard_map(
        per_device,
        mesh=mesh,
        in_specs=(P("ch", "ta"), P(), P()),
        out_specs=P("ch", "ta"),
        check_vma=False,
    )
```

```python
import math

import jax
import jax.numpy as jnp
from jax import lax
from jax.experimental import pallas as pl
from jax.experimental.pallas import tpu as pltpu
from jax.sharding import PartitionSpec as P

TAPS = 129
GAUGE = 4
STRIDE = 128
RANK = 16
ITERS = 6
WIN = 512


def with_halo(block, sides, width):
    for axis, dim in sides:
        count = lax.axis_size(axis)
        forward = [(i, i + 1) for i in range(count - 1)]
        backward = [(target, source) for source, target in forward]
        low = lax.ppermute(
            lax.slice_in_dim(block, block.shape[dim] - width, None, axis=dim), axis, forward
        )
        high = lax.ppermute(lax.slice_in_dim(block, 0, width, axis=dim), axis, backward)
        block = jnp.concatenate([low, block, high], axis=dim)
    return block


def shifted(value, axis, steps):
    count = lax.axis_size(axis)
    first, last = (max(0, -steps), min(count, count - steps))
    return lax.ppermute(value, axis, [(source, source + steps) for source in range(first, last)])


def diagonal(value, dc, dt):
    chs, count = lax.axis_size("ch"), lax.axis_size("ta")
    pairs = [
        (c * count + t, (c + dc) * count + t + dt)
        for c in range(chs) for t in range(count)
        if 0 <= c + dc < chs and 0 <= t + dt < count
    ]
    return lax.ppermute(value, ("ch", "ta"), pairs)


def toeplitz_band(taps, width):
    count = taps.shape[0]
    line = jnp.concatenate([taps, jnp.zeros((width,), taps.dtype)])
    flat = jnp.tile(line, width)[: width * (count + width - 1)]
    return flat.reshape(width, count + width - 1).T


def gram(a, b):
    return lax.dot_general(a, b, (((1,), (1,)), ((), ())), preferred_element_type=jnp.float32)


def orthonormal_rows(image, rows, lanes):
    rank = image.shape[0]
    gram_mat = lax.dot_general(
        image, image, (((1,), (1,)), ((), ())), precision=lax.Precision.HIGHEST,
        preferred_element_type=jnp.float32,
    )
    result = image
    for j in range(rank):
        column = jnp.sum(jnp.where(lanes == j, gram_mat, 0.0), axis=1, keepdims=True)
        scale = 1.0 / jnp.sqrt(column[j : j + 1, :])
        factor = column * scale
        pivot_row = gram_mat[j : j + 1, :] * scale
        image_row = result[j : j + 1, :] * scale
        below = rows > j
        gram_mat = jnp.where(below, gram_mat - factor * pivot_row, gram_mat)
        result = jnp.where(below, result - factor * image_row, jnp.where(rows == j, image_row, result))
    return result


def subspace_kernel(band_ref, start_ref, out_ref):
    windows = out_ref.shape[0]
    rank, win = start_ref.shape
    rows = lax.broadcasted_iota(jnp.int32, (rank, 1), 0)
    lanes = lax.broadcasted_iota(jnp.int32, (rank, rank), 1)
    bases = [start_ref[...] for _ in range(windows)]
    for sweep in range(ITERS):
        for number in range(windows):
            lo = number * STRIDE
            scatter_mat = band_ref[lo : lo + win, lo : lo + win]
            image = jnp.dot(
                bases[number], scatter_mat, precision=lax.Precision.HIGHEST,
                preferred_element_type=jnp.float32,
            )
            bases[number] = orthonormal_rows(image, rows, lanes)
    for number in range(windows):
        out_ref[number] = bases[number].astype(out_ref.dtype)


def subspace(band, start_t, windows):
    return pl.pallas_call(
        subspace_kernel,
        out_shape=jax.ShapeDtypeStruct((windows,) + start_t.shape, jnp.bfloat16),
        in_specs=[
            pl.BlockSpec(memory_space=pltpu.VMEM),
            pl.BlockSpec(memory_space=pltpu.VMEM),
        ],
        out_specs=pl.BlockSpec(memory_space=pltpu.VMEM),
    )(band, start_t)


def fir_kernel(left_ref, right_ref, prev_ref, cur_ref, next_ref, lo_ref, mid_ref, hi_ref, out_ref, *, first, last):
    block = (pl.program_id(0) + first) % (last + 1)
    before = jnp.where(block == 0, left_ref[...], prev_ref[...])
    after = jnp.where(block == last, right_ref[...], next_ref[...])
    out_ref[...] = (
        jnp.dot(before, lo_ref[...], preferred_element_type=jnp.float32)
        + jnp.dot(cur_ref[...], mid_ref[...], preferred_element_type=jnp.float32)
        + jnp.dot(after, hi_ref[...], preferred_element_type=jnp.float32)
    )


def fir(raw, left, right, band, start, length):
    chans, samples = raw.shape
    width = band.shape[1]
    edge = 128
    step = width // edge
    first = start // width
    blocks = samples // width
    lo, mid, hi = band[:edge], band[edge : edge + width], band[edge + width :]
    kernel = lambda *refs: fir_kernel(*refs, first=first, last=blocks - 1)
    full = lambda b: (0, 0)
    at = lambda b: (b + first) % blocks
    return pl.pallas_call(
        kernel,
        grid=(length // width,),
        out_shape=jax.ShapeDtypeStruct((chans, length), jnp.float32),
        in_specs=[
            pl.BlockSpec((chans, edge), full),
            pl.BlockSpec((chans, edge), full),
            pl.BlockSpec((chans, edge), lambda b: (0, jnp.maximum(at(b) * step - 1, 0))),
            pl.BlockSpec((chans, width), lambda b: (0, at(b))),
            pl.BlockSpec((chans, edge), lambda b: (0, jnp.minimum((at(b) + 1) * step, samples // edge - 1))),
            pl.BlockSpec((edge, width), full),
            pl.BlockSpec((width, width), full),
            pl.BlockSpec((edge, width), full),
        ],
        out_specs=pl.BlockSpec((chans, width), lambda b: (0, b)),
    )(left, right, raw, raw, raw, lo, mid, hi)


def clean_kernel(lower_ref, own_ref, upper_ref, basis_ref, middle_ref, *rest):
    out_ref = rest[-1]
    tiles = own_ref.shape[0] // STRIDE
    parts = [lower_ref[k * STRIDE : (k + 1) * STRIDE] for k in range(2)]
    parts += [own_ref[k * STRIDE : (k + 1) * STRIDE] for k in range(tiles)]
    parts.append(upper_ref[...])
    for number in range(tiles):
        coeffs = jnp.dot(basis_ref[number, :, 0:STRIDE], parts[number], preferred_element_type=jnp.float32)
        for k in range(1, WIN // STRIDE):
            coeffs = coeffs + jnp.dot(
                basis_ref[number, :, k * STRIDE : (k + 1) * STRIDE], parts[number + k],
                preferred_element_type=jnp.float32,
            )
        fitted = jnp.dot(
            middle_ref[number], coeffs.astype(jnp.bfloat16), preferred_element_type=jnp.float32
        )
        out_ref[number * STRIDE : (number + 1) * STRIDE] = (
            parts[number + 2].astype(jnp.float32) - fitted
        ).astype(out_ref.dtype)


def clean(lower, own, upper, rounded, total, start, into):
    chans, samples = own.shape
    width = math.gcd(math.gcd(samples, start) if start else samples, 512)
    first = start // width
    middle = jnp.swapaxes(rounded[:, :, 2 * STRIDE : 3 * STRIDE], 1, 2)
    return pl.pallas_call(
        clean_kernel,
        grid=(samples // width,),
        out_shape=jax.ShapeDtypeStruct((chans, total), own.dtype),
        in_specs=[
            pl.BlockSpec((lower.shape[0], width), lambda b: (0, b)),
            pl.BlockSpec((chans, width), lambda b: (0, b)),
            pl.BlockSpec((STRIDE, width), lambda b: (0, b)),
            pl.BlockSpec(rounded.shape, lambda b: (0, 0, 0)),
            pl.BlockSpec(middle.shape, lambda b: (0, 0, 0)),
        ] + ([] if into is None else [pl.BlockSpec(memory_space=pl.ANY)]),
        out_specs=pl.BlockSpec((chans, width), lambda b: (0, (b + first) % (total // width))),
        input_output_aliases={} if into is None else {5: 0},
    )(lower, own, upper, rounded, middle, *([] if into is None else [into]))


def ta_sum(value):
    count = lax.axis_size("ta")
    if count != 4:
        return lax.psum(value, "ta")
    core = lax.axis_index("ta") % 2
    rows = value.shape[0] // 2
    low, high = value[:rows], value[rows:]
    mine = jnp.where(core == 0, low, high)
    theirs = jnp.where(core == 0, high, low)
    partner = [(i, i ^ 1) for i in range(count)]
    across = [(i, i ^ 2) for i in range(count)]
    part = mine + lax.ppermute(theirs, "ta", partner)
    part = part + lax.ppermute(part, "ta", across)
    other = lax.ppermute(part, "ta", partner)
    return jnp.where(core == 0, jnp.concatenate([part, other]), jnp.concatenate([other, part]))


def per_device(raw, fir_taps, start_basis):
    chans = raw.shape[0]
    samples = raw.shape[1]
    half = (TAPS - 1) // 2
    count = lax.axis_size("ta")
    forward = [(i, i + 1) for i in range(count - 1)]
    backward = [(target, source) for source, target in forward]
    blank = jnp.zeros((chans, STRIDE - half), raw.dtype)
    left = jnp.concatenate([blank, lax.ppermute(raw[:, samples - half :], "ta", forward)], axis=1)
    right = jnp.concatenate([lax.ppermute(raw[:, :half], "ta", backward), blank], axis=1)
    edge_rows = jnp.concatenate(
        [shifted(raw[chans - GAUGE :], "ch", 1), shifted(raw[:GAUGE], "ch", -1)], axis=0
    )
    corner = lambda rows, cols, dc, dt: diagonal(raw[rows, cols], dc, dt)
    tail_cols, head_cols = slice(samples - half, None), slice(0, half)
    last_rows, first_rows = slice(chans - GAUGE, None), slice(0, GAUGE)
    edge_blank = jnp.zeros((2 * GAUGE, STRIDE - half), raw.dtype)
    edge_left = jnp.concatenate(
        [edge_blank, jnp.concatenate(
            [corner(last_rows, tail_cols, 1, 1), corner(first_rows, tail_cols, -1, 1)], axis=0)], axis=1
    )
    edge_right = jnp.concatenate(
        [jnp.concatenate(
            [corner(last_rows, head_cols, 1, -1), corner(first_rows, head_cols, -1, -1)], axis=0),
         edge_blank], axis=1
    )
    width = math.gcd(samples, 512)
    band = jnp.pad(toeplitz_band(fir_taps, width), ((half, half), (0, 0)))
    chunks = 2 if samples % 1024 == 0 else 1
    piece = samples // chunks
    tiles = chans // STRIDE
    windows = tiles
    total_time = samples * lax.axis_size("ta")
    gaugeds, lowers, uppers = [], [], []
    own = cross_left = cross_right = None
    filters = []
    for number in range(chunks):
        start = number * piece + width
        wraps = number == chunks - 1
        edges = (left, right) if wraps else (raw[:, :STRIDE], raw[:, :STRIDE])
        outer = (edge_left, edge_right) if wraps else (edge_rows[:, :STRIDE], edge_rows[:, :STRIDE])
        filters.append((fir(raw, *edges, band, start, piece), fir(edge_rows, *outer, band, start, piece)))
    filters = lax.optimization_barrier(filters)
    for number in range(chunks):
        inner, outer = filters[number]
        extended = jnp.concatenate([outer[:GAUGE], inner, outer[GAUGE:]], axis=0)
        gauged = (extended[2 * GAUGE :] - extended[: -2 * GAUGE]).astype(jnp.bfloat16)
        lower_part = shifted(gauged[chans - 2 * STRIDE :], "ch", 1)
        upper_part = shifted(gauged[:STRIDE], "ch", -1)
        local = gram(gauged, gauged)
        own = local if own is None else own + local
        gaugeds.append(gauged)
        lowers.append(lower_part)
        uppers.append(upper_part)

    own = ta_sum(own)
    own_left = shifted(own[chans - 2 * STRIDE :, chans - 2 * STRIDE :], "ch", 1)
    own_right = shifted(own[:STRIDE, :STRIDE], "ch", -1)
    own, lowers, uppers = lax.optimization_barrier((own, lowers, uppers))

    for number in range(chunks):
        lower_part, gauged, upper_part = lowers[number], gaugeds[number], uppers[number]
        left = gram(lower_part, gauged)
        tail = jnp.concatenate([lower_part[STRIDE:], gauged], axis=0)
        right = gram(tail, upper_part)
        cross_left = left if cross_left is None else cross_left + left
        cross_right = right if cross_right is None else cross_right + right

    packed = ta_sum(jnp.concatenate([cross_left[:, :STRIDE], cross_left[:, STRIDE:], cross_right], axis=0))
    tiles_left = 2 * STRIDE
    cross_left = jnp.concatenate(
        [packed[:tiles_left], packed[tiles_left : 2 * tiles_left]], axis=1
    )
    cross_right = packed[2 * tiles_left :]

    zeros = jnp.zeros((STRIDE, STRIDE), jnp.float32)
    top = jnp.concatenate(
        [own_left, cross_left, jnp.concatenate([zeros, cross_right[:STRIDE]], axis=0)], axis=1
    )
    middle = jnp.concatenate(
        [cross_left.T, own, cross_right[STRIDE:]], axis=1
    )
    corner = jnp.concatenate([zeros, cross_right[:STRIDE].T], axis=1)
    bottom = jnp.concatenate([corner, cross_right[STRIDE:].T, own_right], axis=1)
    band = jnp.concatenate([top, middle, bottom], axis=0) / total_time

    rounded = subspace(band, start_basis.T, windows)
    cleaned = None
    for number in range(chunks):
        cleaned = clean(
            lowers[number], gaugeds[number], uppers[number], rounded, samples, number * piece + width, cleaned
        )
    return cleaned


def solution(mesh):
    return jax.shard_map(
        per_device,
        mesh=mesh,
        in_specs=(P("ch", "ta"), P(), P()),
        out_specs=P("ch", "ta"),
        check_vma=False,
    )
```

```python
import math

import jax
import jax.numpy as jnp
from jax import lax
from jax.experimental import pallas as pl
from jax.experimental.pallas import tpu as pltpu
from jax.sharding import PartitionSpec as P

TAPS = 129
GAUGE = 4
STRIDE = 128
RANK = 16
ITERS = 6
WIN = 512


def with_halo(block, sides, width):
    for axis, dim in sides:
        count = lax.axis_size(axis)
        forward = [(i, i + 1) for i in range(count - 1)]
        backward = [(target, source) for source, target in forward]
        low = lax.ppermute(
            lax.slice_in_dim(block, block.shape[dim] - width, None, axis=dim), axis, forward
        )
        high = lax.ppermute(lax.slice_in_dim(block, 0, width, axis=dim), axis, backward)
        block = jnp.concatenate([low, block, high], axis=dim)
    return block


def shifted(value, axis, steps):
    count = lax.axis_size(axis)
    first, last = (max(0, -steps), min(count, count - steps))
    return lax.ppermute(value, axis, [(source, source + steps) for source in range(first, last)])


def toeplitz_band(taps, width):
    count = taps.shape[0]
    line = jnp.concatenate([taps, jnp.zeros((width,), taps.dtype)])
    flat = jnp.tile(line, width)[: width * (count + width - 1)]
    return flat.reshape(width, count + width - 1).T


def gram(a, b):
    return lax.dot_general(a, b, (((1,), (1,)), ((), ())), preferred_element_type=jnp.float32)


def orthonormal_rows(images, rank, rows, lanes):
    windows = len(images)
    gram_mat = jnp.concatenate([
        lax.dot_general(
            image, image, (((1,), (1,)), ((), ())), precision=lax.Precision.HIGHEST,
            preferred_element_type=jnp.float32,
        )
        for image in images
    ], axis=0)
    result = jnp.concatenate(images, axis=0)
    local = rows % rank
    owner = rows // rank

    def pick(value, j):
        picked = value[j : j + 1]
        for number in range(1, windows):
            at = number * rank + j
            picked = jnp.where(owner == number, value[at : at + 1], picked)
        return picked

    for j in range(rank):
        column = jnp.sum(jnp.where(lanes == j, gram_mat, 0.0), axis=1, keepdims=True)
        scale = 1.0 / jnp.sqrt(pick(column, j))
        factor = column * scale
        pivot_row = pick(gram_mat, j) * scale
        image_row = pick(result, j) * scale
        below = local > j
        gram_mat = jnp.where(below, gram_mat - factor * pivot_row, gram_mat)
        result = jnp.where(below, result - factor * image_row, jnp.where(local == j, image_row, result))
    return [result[number * rank : (number + 1) * rank] for number in range(windows)]


def subspace_kernel(band_ref, start_ref, out_ref):
    windows = out_ref.shape[0]
    rank, win = start_ref.shape
    rows = lax.broadcasted_iota(jnp.int32, (windows * rank, 1), 0)
    lanes = lax.broadcasted_iota(jnp.int32, (windows * rank, rank), 1)
    bases = [start_ref[...] for _ in range(windows)]
    for sweep in range(ITERS):
        images = []
        for number in range(windows):
            lo = number * STRIDE
            scatter_mat = band_ref[lo : lo + win, lo : lo + win]
            images.append(jnp.dot(
                bases[number], scatter_mat, precision=lax.Precision.HIGHEST,
                preferred_element_type=jnp.float32,
            ))
        bases = orthonormal_rows(images, rank, rows, lanes)
    for number in range(windows):
        out_ref[number] = bases[number].astype(out_ref.dtype)


def subspace(band, start_t, windows):
    return pl.pallas_call(
        subspace_kernel,
        out_shape=jax.ShapeDtypeStruct((windows,) + start_t.shape, jnp.bfloat16),
        in_specs=[
            pl.BlockSpec(memory_space=pltpu.VMEM),
            pl.BlockSpec(memory_space=pltpu.VMEM),
        ],
        out_specs=pl.BlockSpec(memory_space=pltpu.VMEM),
    )(band, start_t)


def fir_kernel(left_ref, right_ref, prev_ref, cur_ref, next_ref, lo_ref, mid_ref, hi_ref, out_ref, *, first, last):
    block = (pl.program_id(0) + first) % (last + 1)
    before = jnp.where(block == 0, left_ref[...], prev_ref[...])
    after = jnp.where(block == last, right_ref[...], next_ref[...])
    out_ref[...] = (
        jnp.dot(before, lo_ref[...], preferred_element_type=jnp.float32)
        + jnp.dot(cur_ref[...], mid_ref[...], preferred_element_type=jnp.float32)
        + jnp.dot(after, hi_ref[...], preferred_element_type=jnp.float32)
    )


def fir(raw, left, right, band, start, length):
    chans, samples = raw.shape
    width = band.shape[1]
    edge = 128
    step = width // edge
    first = start // width
    blocks = samples // width
    lo, mid, hi = band[:edge], band[edge : edge + width], band[edge + width :]
    kernel = lambda *refs: fir_kernel(*refs, first=first, last=blocks - 1)
    full = lambda b: (0, 0)
    at = lambda b: (b + first) % blocks
    return pl.pallas_call(
        kernel,
        grid=(length // width,),
        out_shape=jax.ShapeDtypeStruct((chans, length), jnp.float32),
        in_specs=[
            pl.BlockSpec((chans, edge), full),
            pl.BlockSpec((chans, edge), full),
            pl.BlockSpec((chans, edge), lambda b: (0, jnp.maximum(at(b) * step - 1, 0))),
            pl.BlockSpec((chans, width), lambda b: (0, at(b))),
            pl.BlockSpec((chans, edge), lambda b: (0, jnp.minimum((at(b) + 1) * step, samples // edge - 1))),
            pl.BlockSpec((edge, width), full),
            pl.BlockSpec((width, width), full),
            pl.BlockSpec((edge, width), full),
        ],
        out_specs=pl.BlockSpec((chans, width), lambda b: (0, b)),
    )(left, right, raw, raw, raw, lo, mid, hi)


def clean_kernel(lower_ref, own_ref, upper_ref, basis_ref, middle_ref, *rest):
    out_ref = rest[-1]
    tiles = own_ref.shape[0] // STRIDE
    parts = [lower_ref[k * STRIDE : (k + 1) * STRIDE] for k in range(2)]
    parts += [own_ref[k * STRIDE : (k + 1) * STRIDE] for k in range(tiles)]
    parts.append(upper_ref[...])
    for number in range(tiles):
        coeffs = jnp.dot(basis_ref[number, :, 0:STRIDE], parts[number], preferred_element_type=jnp.float32)
        for k in range(1, WIN // STRIDE):
            coeffs = coeffs + jnp.dot(
                basis_ref[number, :, k * STRIDE : (k + 1) * STRIDE], parts[number + k],
                preferred_element_type=jnp.float32,
            )
        fitted = jnp.dot(
            middle_ref[number], coeffs.astype(jnp.bfloat16), preferred_element_type=jnp.float32
        )
        out_ref[number * STRIDE : (number + 1) * STRIDE] = (
            parts[number + 2].astype(jnp.float32) - fitted
        ).astype(out_ref.dtype)


def clean(lower, own, upper, rounded, total, start, into):
    chans, samples = own.shape
    width = math.gcd(math.gcd(samples, start) if start else samples, 512)
    first = start // width
    middle = jnp.swapaxes(rounded[:, :, 2 * STRIDE : 3 * STRIDE], 1, 2)
    return pl.pallas_call(
        clean_kernel,
        grid=(samples // width,),
        out_shape=jax.ShapeDtypeStruct((chans, total), own.dtype),
        in_specs=[
            pl.BlockSpec((lower.shape[0], width), lambda b: (0, b)),
            pl.BlockSpec((chans, width), lambda b: (0, b)),
            pl.BlockSpec((STRIDE, width), lambda b: (0, b)),
            pl.BlockSpec(rounded.shape, lambda b: (0, 0, 0)),
            pl.BlockSpec(middle.shape, lambda b: (0, 0, 0)),
        ] + ([] if into is None else [pl.BlockSpec(memory_space=pl.ANY)]),
        out_specs=pl.BlockSpec((chans, width), lambda b: (0, (b + first) % (total // width))),
        input_output_aliases={} if into is None else {5: 0},
    )(lower, own, upper, rounded, middle, *([] if into is None else [into]))


def ta_sum(value):
    count = lax.axis_size("ta")
    if count != 4:
        return lax.psum(value, "ta")
    core = lax.axis_index("ta") % 2
    rows = value.shape[0] // 2
    low, high = value[:rows], value[rows:]
    mine = jnp.where(core == 0, low, high)
    theirs = jnp.where(core == 0, high, low)
    partner = [(i, i ^ 1) for i in range(count)]
    across = [(i, i ^ 2) for i in range(count)]
    part = mine + lax.ppermute(theirs, "ta", partner)
    part = part + lax.ppermute(part, "ta", across)
    other = lax.ppermute(part, "ta", partner)
    return jnp.where(core == 0, jnp.concatenate([part, other]), jnp.concatenate([other, part]))


def per_device(raw, fir_taps, start_basis):
    chans = raw.shape[0]
    samples = raw.shape[1]
    half = (TAPS - 1) // 2
    count = lax.axis_size("ta")
    forward = [(i, i + 1) for i in range(count - 1)]
    backward = [(target, source) for source, target in forward]
    blank = jnp.zeros((chans, STRIDE - half), raw.dtype)
    left = jnp.concatenate([blank, lax.ppermute(raw[:, samples - half :], "ta", forward)], axis=1)
    right = jnp.concatenate([lax.ppermute(raw[:, :half], "ta", backward), blank], axis=1)
    width = math.gcd(samples, 512)
    band = jnp.pad(toeplitz_band(fir_taps, width), ((half, half), (0, 0)))
    chunks = 2 if samples % 1024 == 0 else 1
    piece = samples // chunks
    tiles = chans // STRIDE
    windows = tiles
    total_time = samples * lax.axis_size("ta")
    gaugeds, lowers, uppers = [], [], []
    own = cross_left = cross_right = None
    filters = []
    for number in range(chunks):
        start = number * piece + width
        edges = (left, right) if number == chunks - 1 else (raw[:, :STRIDE], raw[:, :STRIDE])
        filters.append(fir(raw, *edges, band, start, piece))
    filters = lax.optimization_barrier(filters)
    for number in range(chunks):
        extended = with_halo(filters[number], (("ch", 0),), GAUGE)
        gauged = (extended[2 * GAUGE :] - extended[: -2 * GAUGE]).astype(jnp.bfloat16)
        lower_part = shifted(gauged[chans - 2 * STRIDE :], "ch", 1)
        upper_part = shifted(gauged[:STRIDE], "ch", -1)
        local = gram(gauged, gauged)
        own = local if own is None else own + local
        gaugeds.append(gauged)
        lowers.append(lower_part)
        uppers.append(upper_part)

    own = ta_sum(own)
    own_left = shifted(own[chans - 2 * STRIDE :, chans - 2 * STRIDE :], "ch", 1)
    own_right = shifted(own[:STRIDE, :STRIDE], "ch", -1)
    own, lowers, uppers = lax.optimization_barrier((own, lowers, uppers))

    for number in range(chunks):
        lower_part, gauged, upper_part = lowers[number], gaugeds[number], uppers[number]
        left = gram(lower_part, gauged)
        tail = jnp.concatenate([lower_part[STRIDE:], gauged], axis=0)
        right = gram(tail, upper_part)
        cross_left = left if cross_left is None else cross_left + left
        cross_right = right if cross_right is None else cross_right + right

    packed = ta_sum(jnp.concatenate([cross_left[:, :STRIDE], cross_left[:, STRIDE:], cross_right], axis=0))
    tiles_left = 2 * STRIDE
    cross_left = jnp.concatenate(
        [packed[:tiles_left], packed[tiles_left : 2 * tiles_left]], axis=1
    )
    cross_right = packed[2 * tiles_left :]

    zeros = jnp.zeros((STRIDE, STRIDE), jnp.float32)
    top = jnp.concatenate(
        [own_left, cross_left, jnp.concatenate([zeros, cross_right[:STRIDE]], axis=0)], axis=1
    )
    middle = jnp.concatenate(
        [cross_left.T, own, cross_right[STRIDE:]], axis=1
    )
    corner = jnp.concatenate([zeros, cross_right[:STRIDE].T], axis=1)
    bottom = jnp.concatenate([corner, cross_right[STRIDE:].T, own_right], axis=1)
    band = jnp.concatenate([top, middle, bottom], axis=0) / total_time

    rounded = subspace(band, start_basis.T, windows)
    cleaned = None
    for number in range(chunks):
        cleaned = clean(
            lowers[number], gaugeds[number], uppers[number], rounded, samples, number * piece + width, cleaned
        )
    return cleaned


def solution(mesh):
    return jax.shard_map(
        per_device,
        mesh=mesh,
        in_specs=(P("ch", "ta"), P(), P()),
        out_specs=P("ch", "ta"),
        check_vma=False,
    )
```

```python
import math

import jax
import jax.numpy as jnp
from jax import lax
from jax.experimental import pallas as pl
from jax.experimental.pallas import tpu as pltpu
from jax.sharding import PartitionSpec as P

TAPS = 129
GAUGE = 4
STRIDE = 128
RANK = 16
ITERS = 6
WIN = 512


def with_halo(block, sides, width):
    for axis, dim in sides:
        count = lax.axis_size(axis)
        forward = [(i, i + 1) for i in range(count - 1)]
        backward = [(target, source) for source, target in forward]
        low = lax.ppermute(
            lax.slice_in_dim(block, block.shape[dim] - width, None, axis=dim), axis, forward
        )
        high = lax.ppermute(lax.slice_in_dim(block, 0, width, axis=dim), axis, backward)
        block = jnp.concatenate([low, block, high], axis=dim)
    return block


def shifted(value, axis, steps):
    count = lax.axis_size(axis)
    first, last = (max(0, -steps), min(count, count - steps))
    return lax.ppermute(value, axis, [(source, source + steps) for source in range(first, last)])


def toeplitz_band(taps, width):
    count = taps.shape[0]
    line = jnp.concatenate([taps, jnp.zeros((width,), taps.dtype)])
    flat = jnp.tile(line, width)[: width * (count + width - 1)]
    return flat.reshape(width, count + width - 1).T


def gram(a, b):
    return lax.dot_general(a, b, (((1,), (1,)), ((), ())), preferred_element_type=jnp.float32)


def orthonormal_rows(image, rows, lanes):
    rank = image.shape[0]
    gram_mat = lax.dot_general(
        image, image, (((1,), (1,)), ((), ())), precision=lax.Precision.HIGHEST,
        preferred_element_type=jnp.float32,
    )
    result = image
    for j in range(rank):
        column = jnp.sum(jnp.where(lanes == j, gram_mat, 0.0), axis=1, keepdims=True)
        scale = 1.0 / jnp.sqrt(column[j : j + 1, :])
        factor = column * scale
        pivot_row = gram_mat[j : j + 1, :] * scale
        image_row = result[j : j + 1, :] * scale
        below = rows > j
        gram_mat = jnp.where(below, gram_mat - factor * pivot_row, gram_mat)
        result = jnp.where(below, result - factor * image_row, jnp.where(rows == j, image_row, result))
    return result


def subspace_kernel(band_ref, start_ref, out_ref):
    windows = out_ref.shape[0]
    rank, win = start_ref.shape
    rows = lax.broadcasted_iota(jnp.int32, (rank, 1), 0)
    lanes = lax.broadcasted_iota(jnp.int32, (rank, rank), 1)
    bases = [start_ref[...] for _ in range(windows)]
    for sweep in range(ITERS):
        for number in range(windows):
            lo = number * STRIDE
            scatter_mat = band_ref[lo : lo + win, lo : lo + win]
            image = jnp.dot(
                bases[number], scatter_mat, precision=lax.Precision.HIGHEST,
                preferred_element_type=jnp.float32,
            )
            bases[number] = orthonormal_rows(image, rows, lanes)
    for number in range(windows):
        out_ref[number] = bases[number].astype(out_ref.dtype)


def subspace(band, start_t, windows):
    return pl.pallas_call(
        subspace_kernel,
        out_shape=jax.ShapeDtypeStruct((windows,) + start_t.shape, jnp.bfloat16),
        in_specs=[
            pl.BlockSpec(memory_space=pltpu.VMEM),
            pl.BlockSpec(memory_space=pltpu.VMEM),
        ],
        out_specs=pl.BlockSpec(memory_space=pltpu.VMEM),
    )(band, start_t)


def fir_kernel(left_ref, right_ref, prev_ref, cur_ref, next_ref, lo_ref, mid_ref, hi_ref, out_ref, *, first, last):
    block = (pl.program_id(0) + first) % (last + 1)
    before = jnp.where(block == 0, left_ref[...], prev_ref[...])
    after = jnp.where(block == last, right_ref[...], next_ref[...])
    out_ref[...] = (
        jnp.dot(before, lo_ref[...], preferred_element_type=jnp.float32)
        + jnp.dot(cur_ref[...], mid_ref[...], preferred_element_type=jnp.float32)
        + jnp.dot(after, hi_ref[...], preferred_element_type=jnp.float32)
    )


def fir(raw, left, right, band, start, length):
    chans, samples = raw.shape
    width = band.shape[1]
    edge = 128
    step = width // edge
    first = start // width
    blocks = samples // width
    lo, mid, hi = band[:edge], band[edge : edge + width], band[edge + width :]
    kernel = lambda *refs: fir_kernel(*refs, first=first, last=blocks - 1)
    full = lambda b: (0, 0)
    at = lambda b: (b + first) % blocks
    return pl.pallas_call(
        kernel,
        grid=(length // width,),
        out_shape=jax.ShapeDtypeStruct((chans, length), jnp.float32),
        in_specs=[
            pl.BlockSpec((chans, edge), full),
            pl.BlockSpec((chans, edge), full),
            pl.BlockSpec((chans, edge), lambda b: (0, jnp.maximum(at(b) * step - 1, 0))),
            pl.BlockSpec((chans, width), lambda b: (0, at(b))),
            pl.BlockSpec((chans, edge), lambda b: (0, jnp.minimum((at(b) + 1) * step, samples // edge - 1))),
            pl.BlockSpec((edge, width), full),
            pl.BlockSpec((width, width), full),
            pl.BlockSpec((edge, width), full),
        ],
        out_specs=pl.BlockSpec((chans, width), lambda b: (0, b)),
    )(left, right, raw, raw, raw, lo, mid, hi)


def clean_kernel(lower_ref, own_ref, upper_ref, basis_ref, middle_ref, *rest):
    out_ref = rest[-1]
    tiles = own_ref.shape[0] // STRIDE
    rank = middle_ref.shape[2]
    span = WIN // STRIDE
    parts = [lower_ref[k * STRIDE : (k + 1) * STRIDE] for k in range(2)]
    parts += [own_ref[k * STRIDE : (k + 1) * STRIDE] for k in range(tiles)]
    parts.append(upper_ref[...])
    coeffs = [None] * tiles
    for k in range(len(parts)):
        users = [number for number in range(tiles) if number <= k < number + span]
        product = jnp.dot(basis_ref[k, : len(users) * rank], parts[k], preferred_element_type=jnp.float32)
        for slot, number in enumerate(users):
            piece = product[slot * rank : (slot + 1) * rank]
            coeffs[number] = piece if coeffs[number] is None else coeffs[number] + piece
    for number in range(tiles):
        fitted = jnp.dot(
            middle_ref[number], coeffs[number].astype(jnp.bfloat16), preferred_element_type=jnp.float32
        )
        out_ref[number * STRIDE : (number + 1) * STRIDE] = (
            parts[number + 2].astype(jnp.float32) - fitted
        ).astype(out_ref.dtype)


def stack_basis(rounded):
    windows, rank, win = rounded.shape
    span = win // STRIDE
    stacks = []
    for k in range(windows + span - 1):
        users = [number for number in range(windows) if number <= k < number + span]
        rows = [rounded[number, :, (k - number) * STRIDE : (k - number + 1) * STRIDE] for number in users]
        rows += [jnp.zeros((rank, STRIDE), rounded.dtype)] * (min(windows, span) - len(users))
        stacks.append(jnp.concatenate(rows, axis=0))
    return jnp.stack(stacks)


def clean(lower, own, upper, rounded, total, start, into):
    chans, samples = own.shape
    width = math.gcd(math.gcd(samples, start) if start else samples, 512)
    first = start // width
    middle = jnp.swapaxes(rounded[:, :, 2 * STRIDE : 3 * STRIDE], 1, 2)
    stacked = stack_basis(rounded)
    return pl.pallas_call(
        clean_kernel,
        grid=(samples // width,),
        out_shape=jax.ShapeDtypeStruct((chans, total), own.dtype),
        in_specs=[
            pl.BlockSpec((lower.shape[0], width), lambda b: (0, b)),
            pl.BlockSpec((chans, width), lambda b: (0, b)),
            pl.BlockSpec((STRIDE, width), lambda b: (0, b)),
            pl.BlockSpec(stacked.shape, lambda b: (0, 0, 0)),
            pl.BlockSpec(middle.shape, lambda b: (0, 0, 0)),
        ] + ([] if into is None else [pl.BlockSpec(memory_space=pl.ANY)]),
        out_specs=pl.BlockSpec((chans, width), lambda b: (0, (b + first) % (total // width))),
        input_output_aliases={} if into is None else {5: 0},
    )(lower, own, upper, stacked, middle, *([] if into is None else [into]))


def ta_sum(value):
    count = lax.axis_size("ta")
    if count != 4:
        return lax.psum(value, "ta")
    core = lax.axis_index("ta") % 2
    rows = value.shape[0] // 2
    low, high = value[:rows], value[rows:]
    mine = jnp.where(core == 0, low, high)
    theirs = jnp.where(core == 0, high, low)
    partner = [(i, i ^ 1) for i in range(count)]
    across = [(i, i ^ 2) for i in range(count)]
    part = mine + lax.ppermute(theirs, "ta", partner)
    part = part + lax.ppermute(part, "ta", across)
    other = lax.ppermute(part, "ta", partner)
    return jnp.where(core == 0, jnp.concatenate([part, other]), jnp.concatenate([other, part]))


def per_device(raw, fir_taps, start_basis):
    chans = raw.shape[0]
    samples = raw.shape[1]
    half = (TAPS - 1) // 2
    count = lax.axis_size("ta")
    forward = [(i, i + 1) for i in range(count - 1)]
    backward = [(target, source) for source, target in forward]
    blank = jnp.zeros((chans, STRIDE - half), raw.dtype)
    left = jnp.concatenate([blank, lax.ppermute(raw[:, samples - half :], "ta", forward)], axis=1)
    right = jnp.concatenate([lax.ppermute(raw[:, :half], "ta", backward), blank], axis=1)
    width = math.gcd(samples, 512)
    band = jnp.pad(toeplitz_band(fir_taps, width), ((half, half), (0, 0)))
    chunks = 2 if samples % 1024 == 0 else 1
    piece = samples // chunks
    tiles = chans // STRIDE
    windows = tiles
    total_time = samples * lax.axis_size("ta")
    gaugeds, lowers, uppers = [], [], []
    own = cross_left = cross_right = None
    filters = []
    for number in range(chunks):
        start = number * piece + width
        edges = (left, right) if number == chunks - 1 else (raw[:, :STRIDE], raw[:, :STRIDE])
        filters.append(fir(raw, *edges, band, start, piece))
    filters = lax.optimization_barrier(filters)
    for number in range(chunks):
        extended = with_halo(filters[number], (("ch", 0),), GAUGE)
        gauged = (extended[2 * GAUGE :] - extended[: -2 * GAUGE]).astype(jnp.bfloat16)
        lower_part = shifted(gauged[chans - 2 * STRIDE :], "ch", 1)
        upper_part = shifted(gauged[:STRIDE], "ch", -1)
        local = gram(gauged, gauged)
        own = local if own is None else own + local
        gaugeds.append(gauged)
        lowers.append(lower_part)
        uppers.append(upper_part)

    own = ta_sum(own)
    own_left = shifted(own[chans - 2 * STRIDE :, chans - 2 * STRIDE :], "ch", 1)
    own_right = shifted(own[:STRIDE, :STRIDE], "ch", -1)
    own, lowers, uppers = lax.optimization_barrier((own, lowers, uppers))

    for number in range(chunks):
        lower_part, gauged, upper_part = lowers[number], gaugeds[number], uppers[number]
        left = gram(lower_part, gauged)
        tail = jnp.concatenate([lower_part[STRIDE:], gauged], axis=0)
        right = gram(tail, upper_part)
        cross_left = left if cross_left is None else cross_left + left
        cross_right = right if cross_right is None else cross_right + right

    packed = ta_sum(jnp.concatenate([cross_left[:, :STRIDE], cross_left[:, STRIDE:], cross_right], axis=0))
    tiles_left = 2 * STRIDE
    cross_left = jnp.concatenate(
        [packed[:tiles_left], packed[tiles_left : 2 * tiles_left]], axis=1
    )
    cross_right = packed[2 * tiles_left :]

    zeros = jnp.zeros((STRIDE, STRIDE), jnp.float32)
    top = jnp.concatenate(
        [own_left, cross_left, jnp.concatenate([zeros, cross_right[:STRIDE]], axis=0)], axis=1
    )
    middle = jnp.concatenate(
        [cross_left.T, own, cross_right[STRIDE:]], axis=1
    )
    corner = jnp.concatenate([zeros, cross_right[:STRIDE].T], axis=1)
    bottom = jnp.concatenate([corner, cross_right[STRIDE:].T, own_right], axis=1)
    band = jnp.concatenate([top, middle, bottom], axis=0) / total_time

    rounded = subspace(band, start_basis.T, windows)
    cleaned = None
    for number in range(chunks):
        cleaned = clean(
            lowers[number], gaugeds[number], uppers[number], rounded, samples, number * piece + width, cleaned
        )
    return cleaned


def solution(mesh):
    return jax.shard_map(
        per_device,
        mesh=mesh,
        in_specs=(P("ch", "ta"), P(), P()),
        out_specs=P("ch", "ta"),
        check_vma=False,
    )
```

```python
import math

import jax
import jax.numpy as jnp
from jax import lax
from jax.experimental import pallas as pl
from jax.experimental.pallas import tpu as pltpu
from jax.sharding import PartitionSpec as P

TAPS = 129
GAUGE = 4
STRIDE = 128
RANK = 16
ITERS = 6
WIN = 512


def with_halo(block, sides, width):
    for axis, dim in sides:
        count = lax.axis_size(axis)
        forward = [(i, i + 1) for i in range(count - 1)]
        backward = [(target, source) for source, target in forward]
        low = lax.ppermute(
            lax.slice_in_dim(block, block.shape[dim] - width, None, axis=dim), axis, forward
        )
        high = lax.ppermute(lax.slice_in_dim(block, 0, width, axis=dim), axis, backward)
        block = jnp.concatenate([low, block, high], axis=dim)
    return block


def shifted(value, axis, steps):
    count = lax.axis_size(axis)
    first, last = (max(0, -steps), min(count, count - steps))
    return lax.ppermute(value, axis, [(source, source + steps) for source in range(first, last)])


def toeplitz_band(taps, width):
    count = taps.shape[0]
    line = jnp.concatenate([taps, jnp.zeros((width,), taps.dtype)])
    flat = jnp.tile(line, width)[: width * (count + width - 1)]
    return flat.reshape(width, count + width - 1).T


def gram(a, b):
    return lax.dot_general(a, b, (((1,), (1,)), ((), ())), preferred_element_type=jnp.float32)


def orthonormal_rows(image, rows, lanes):
    rank = image.shape[0]
    gram_mat = lax.dot_general(
        image, image, (((1,), (1,)), ((), ())), precision=lax.Precision.HIGHEST,
        preferred_element_type=jnp.float32,
    )
    result = image
    for j in range(rank):
        column = jnp.sum(jnp.where(lanes == j, gram_mat, 0.0), axis=1, keepdims=True)
        scale = 1.0 / jnp.sqrt(column[j : j + 1, :])
        factor = column * scale
        pivot_row = gram_mat[j : j + 1, :] * scale
        image_row = result[j : j + 1, :] * scale
        below = rows > j
        gram_mat = jnp.where(below, gram_mat - factor * pivot_row, gram_mat)
        result = jnp.where(below, result - factor * image_row, jnp.where(rows == j, image_row, result))
    return result


def subspace_kernel(band_ref, start_ref, out_ref):
    windows = out_ref.shape[0]
    rank, win = start_ref.shape
    rows = lax.broadcasted_iota(jnp.int32, (rank, 1), 0)
    lanes = lax.broadcasted_iota(jnp.int32, (rank, rank), 1)
    bases = [start_ref[...] for _ in range(windows)]
    for sweep in range(ITERS):
        for number in range(windows):
            lo = number * STRIDE
            scatter_mat = band_ref[lo : lo + win, lo : lo + win]
            image = jnp.dot(
                bases[number], scatter_mat, precision=lax.Precision.HIGHEST,
                preferred_element_type=jnp.float32,
            )
            bases[number] = orthonormal_rows(image, rows, lanes)
    for number in range(windows):
        out_ref[number] = bases[number].astype(out_ref.dtype)


def subspace(band, start_t, windows):
    return pl.pallas_call(
        subspace_kernel,
        out_shape=jax.ShapeDtypeStruct((windows,) + start_t.shape, jnp.bfloat16),
        in_specs=[
            pl.BlockSpec(memory_space=pltpu.VMEM),
            pl.BlockSpec(memory_space=pltpu.VMEM),
        ],
        out_specs=pl.BlockSpec(memory_space=pltpu.VMEM),
    )(band, start_t)


def fir_kernel(left_ref, right_ref, prev_ref, cur_ref, next_ref, lo_ref, mid_ref, hi_ref, out_ref, *, first, last):
    block = (pl.program_id(0) + first) % (last + 1)
    before = jnp.where(block == 0, left_ref[...], prev_ref[...])
    after = jnp.where(block == last, right_ref[...], next_ref[...])
    out_ref[...] = (
        jnp.dot(before, lo_ref[...], preferred_element_type=jnp.float32)
        + jnp.dot(cur_ref[...], mid_ref[...], preferred_element_type=jnp.float32)
        + jnp.dot(after, hi_ref[...], preferred_element_type=jnp.float32)
    )


def fir(raw, left, right, band, start, length):
    chans, samples = raw.shape
    width = band.shape[1]
    edge = 128
    step = width // edge
    first = start // width
    blocks = samples // width
    lo, mid, hi = band[:edge], band[edge : edge + width], band[edge + width :]
    kernel = lambda *refs: fir_kernel(*refs, first=first, last=blocks - 1)
    full = lambda b: (0, 0)
    at = lambda b: (b + first) % blocks
    return pl.pallas_call(
        kernel,
        grid=(length // width,),
        out_shape=jax.ShapeDtypeStruct((chans, length), jnp.float32),
        in_specs=[
            pl.BlockSpec((chans, edge), full),
            pl.BlockSpec((chans, edge), full),
            pl.BlockSpec((chans, edge), lambda b: (0, jnp.maximum(at(b) * step - 1, 0))),
            pl.BlockSpec((chans, width), lambda b: (0, at(b))),
            pl.BlockSpec((chans, edge), lambda b: (0, jnp.minimum((at(b) + 1) * step, samples // edge - 1))),
            pl.BlockSpec((edge, width), full),
            pl.BlockSpec((width, width), full),
            pl.BlockSpec((edge, width), full),
        ],
        out_specs=pl.BlockSpec((chans, width), lambda b: (0, b)),
    )(left, right, raw, raw, raw, lo, mid, hi)


def clean_kernel(lower_ref, own_ref, upper_ref, basis_ref, middle_ref, *rest):
    out_ref = rest[-1]
    tiles = own_ref.shape[0] // STRIDE
    parts = [lower_ref[k * STRIDE : (k + 1) * STRIDE] for k in range(2)]
    parts += [own_ref[k * STRIDE : (k + 1) * STRIDE] for k in range(tiles)]
    parts.append(upper_ref[...])
    for number in range(tiles):
        coeffs = jnp.dot(basis_ref[number, :, 0:STRIDE], parts[number], preferred_element_type=jnp.float32)
        for k in range(1, WIN // STRIDE):
            coeffs = coeffs + jnp.dot(
                basis_ref[number, :, k * STRIDE : (k + 1) * STRIDE], parts[number + k],
                preferred_element_type=jnp.float32,
            )
        fitted = jnp.dot(
            middle_ref[number], coeffs.astype(jnp.bfloat16), preferred_element_type=jnp.float32
        )
        out_ref[number * STRIDE : (number + 1) * STRIDE] = (
            parts[number + 2].astype(jnp.float32) - fitted
        ).astype(out_ref.dtype)


def clean(lower, own, upper, rounded, total, start, into):
    chans, samples = own.shape
    width = math.gcd(math.gcd(samples, start) if start else samples, 512)
    first = start // width
    middle = jnp.swapaxes(rounded[:, :, 2 * STRIDE : 3 * STRIDE], 1, 2)
    return pl.pallas_call(
        clean_kernel,
        grid=(samples // width,),
        out_shape=jax.ShapeDtypeStruct((chans, total), own.dtype),
        in_specs=[
            pl.BlockSpec((lower.shape[0], width), lambda b: (0, b)),
            pl.BlockSpec((chans, width), lambda b: (0, b)),
            pl.BlockSpec((STRIDE, width), lambda b: (0, b)),
            pl.BlockSpec(rounded.shape, lambda b: (0, 0, 0)),
            pl.BlockSpec(middle.shape, lambda b: (0, 0, 0)),
        ] + ([] if into is None else [pl.BlockSpec(memory_space=pl.ANY)]),
        out_specs=pl.BlockSpec((chans, width), lambda b: (0, (b + first) % (total // width))),
        input_output_aliases={} if into is None else {5: 0},
    )(lower, own, upper, rounded, middle, *([] if into is None else [into]))


def ta_sum(value):
    count = lax.axis_size("ta")
    if count != 4:
        return lax.psum(value, "ta")
    core = lax.axis_index("ta") % 2
    rows = value.shape[0] // 2
    low, high = value[:rows], value[rows:]
    mine = jnp.where(core == 0, low, high)
    theirs = jnp.where(core == 0, high, low)
    partner = [(i, i ^ 1) for i in range(count)]
    across = [(i, i ^ 2) for i in range(count)]
    part = mine + lax.ppermute(theirs, "ta", partner)
    part = part + lax.ppermute(part, "ta", across)
    other = lax.ppermute(part, "ta", partner)
    return jnp.where(core == 0, jnp.concatenate([part, other]), jnp.concatenate([other, part]))


def per_device(raw, fir_taps, start_basis):
    chans = raw.shape[0]
    samples = raw.shape[1]
    half = (TAPS - 1) // 2
    count = lax.axis_size("ta")
    forward = [(i, i + 1) for i in range(count - 1)]
    backward = [(target, source) for source, target in forward]
    blank = jnp.zeros((chans, STRIDE - half), raw.dtype)
    left = jnp.concatenate([blank, lax.ppermute(raw[:, samples - half :], "ta", forward)], axis=1)
    right = jnp.concatenate([lax.ppermute(raw[:, :half], "ta", backward), blank], axis=1)
    width = math.gcd(samples, 512)
    band = jnp.pad(toeplitz_band(fir_taps, width), ((half, half), (0, 0)))
    chunks = 2 if samples % 1024 == 0 else 1
    piece = samples // chunks
    tiles = chans // STRIDE
    windows = tiles
    total_time = samples * lax.axis_size("ta")
    gaugeds, lowers, uppers = [], [], []
    own = cross_left = cross_right = None
    rimmed = jnp.concatenate(
        [shifted(raw[chans - GAUGE :], "ch", 1), raw, shifted(raw[:GAUGE], "ch", -1)], axis=0
    )
    filters = []
    for number in range(chunks):
        start = number * piece + width
        if number == chunks - 1:
            filters.append(fir(raw, left, right, band, start, piece))
        else:
            filters.append(fir(rimmed, rimmed[:, :STRIDE], rimmed[:, :STRIDE], band, start, piece))
    filters = lax.optimization_barrier(filters)
    for number in range(chunks):
        if number == chunks - 1:
            extended = with_halo(filters[number], (("ch", 0),), GAUGE)
        else:
            extended = filters[number]
        gauged = (extended[2 * GAUGE :] - extended[: -2 * GAUGE]).astype(jnp.bfloat16)
        lower_part = shifted(gauged[chans - 2 * STRIDE :], "ch", 1)
        upper_part = shifted(gauged[:STRIDE], "ch", -1)
        local = gram(gauged, gauged)
        own = local if own is None else own + local
        gaugeds.append(gauged)
        lowers.append(lower_part)
        uppers.append(upper_part)

    own = ta_sum(own)
    own_left = shifted(own[chans - 2 * STRIDE :, chans - 2 * STRIDE :], "ch", 1)
    own_right = shifted(own[:STRIDE, :STRIDE], "ch", -1)
    own, lowers, uppers = lax.optimization_barrier((own, lowers, uppers))

    for number in range(chunks):
        lower_part, gauged, upper_part = lowers[number], gaugeds[number], uppers[number]
        left = gram(lower_part, gauged)
        tail = jnp.concatenate([lower_part[STRIDE:], gauged], axis=0)
        right = gram(tail, upper_part)
        cross_left = left if cross_left is None else cross_left + left
        cross_right = right if cross_right is None else cross_right + right

    packed = ta_sum(jnp.concatenate([cross_left[:, :STRIDE], cross_left[:, STRIDE:], cross_right], axis=0))
    tiles_left = 2 * STRIDE
    cross_left = jnp.concatenate(
        [packed[:tiles_left], packed[tiles_left : 2 * tiles_left]], axis=1
    )
    cross_right = packed[2 * tiles_left :]

    zeros = jnp.zeros((STRIDE, STRIDE), jnp.float32)
    top = jnp.concatenate(
        [own_left, cross_left, jnp.concatenate([zeros, cross_right[:STRIDE]], axis=0)], axis=1
    )
    middle = jnp.concatenate(
        [cross_left.T, own, cross_right[STRIDE:]], axis=1
    )
    corner = jnp.concatenate([zeros, cross_right[:STRIDE].T], axis=1)
    bottom = jnp.concatenate([corner, cross_right[STRIDE:].T, own_right], axis=1)
    band = jnp.concatenate([top, middle, bottom], axis=0) / total_time

    rounded = subspace(band, start_basis.T, windows)
    cleaned = None
    for number in range(chunks):
        cleaned = clean(
            lowers[number], gaugeds[number], uppers[number], rounded, samples, number * piece + width, cleaned
        )
    return cleaned


def solution(mesh):
    return jax.shard_map(
        per_device,
        mesh=mesh,
        in_specs=(P("ch", "ta"), P(), P()),
        out_specs=P("ch", "ta"),
        check_vma=False,
    )
```

```python
import math

import jax
import jax.numpy as jnp
from jax import lax
from jax.experimental import pallas as pl
from jax.experimental.pallas import tpu as pltpu
from jax.sharding import PartitionSpec as P

TAPS = 129
GAUGE = 4
STRIDE = 128
RANK = 16
ITERS = 6
WIN = 512


def with_halo(block, sides, width):
    for axis, dim in sides:
        count = lax.axis_size(axis)
        forward = [(i, i + 1) for i in range(count - 1)]
        backward = [(target, source) for source, target in forward]
        low = lax.ppermute(
            lax.slice_in_dim(block, block.shape[dim] - width, None, axis=dim), axis, forward
        )
        high = lax.ppermute(lax.slice_in_dim(block, 0, width, axis=dim), axis, backward)
        block = jnp.concatenate([low, block, high], axis=dim)
    return block


def shifted(value, axis, steps):
    count = lax.axis_size(axis)
    first, last = (max(0, -steps), min(count, count - steps))
    return lax.ppermute(value, axis, [(source, source + steps) for source in range(first, last)])


def toeplitz_band(taps, width):
    count = taps.shape[0]
    line = jnp.concatenate([taps, jnp.zeros((width,), taps.dtype)])
    flat = jnp.tile(line, width)[: width * (count + width - 1)]
    return flat.reshape(width, count + width - 1).T


def gram(a, b):
    return lax.dot_general(a, b, (((1,), (1,)), ((), ())), preferred_element_type=jnp.float32)


def orthonormal_rows(image, rows, lanes):
    rank = image.shape[0]
    gram_mat = lax.dot_general(
        image, image, (((1,), (1,)), ((), ())), precision=lax.Precision.HIGHEST,
        preferred_element_type=jnp.float32,
    )
    result = image
    for j in range(rank):
        column = jnp.sum(jnp.where(lanes == j, gram_mat, 0.0), axis=1, keepdims=True)
        scale = 1.0 / jnp.sqrt(column[j : j + 1, :])
        factor = column * scale
        pivot_row = gram_mat[j : j + 1, :] * scale
        image_row = result[j : j + 1, :] * scale
        below = rows > j
        gram_mat = jnp.where(below, gram_mat - factor * pivot_row, gram_mat)
        result = jnp.where(below, result - factor * image_row, jnp.where(rows == j, image_row, result))
    return result


def subspace_kernel(band_ref, start_ref, out_ref):
    windows = out_ref.shape[0]
    rank, win = start_ref.shape
    rows = lax.broadcasted_iota(jnp.int32, (rank, 1), 0)
    lanes = lax.broadcasted_iota(jnp.int32, (rank, rank), 1)
    bases = [start_ref[...] for _ in range(windows)]
    for sweep in range(ITERS):
        for number in range(windows):
            lo = number * STRIDE
            scatter_mat = band_ref[lo : lo + win, lo : lo + win]
            image = jnp.dot(
                bases[number], scatter_mat, precision=lax.Precision.HIGHEST,
                preferred_element_type=jnp.float32,
            )
            bases[number] = orthonormal_rows(image, rows, lanes)
    for number in range(windows):
        out_ref[number] = bases[number].astype(out_ref.dtype)


def subspace(band, start_t, windows):
    return pl.pallas_call(
        subspace_kernel,
        out_shape=jax.ShapeDtypeStruct((windows,) + start_t.shape, jnp.bfloat16),
        in_specs=[
            pl.BlockSpec(memory_space=pltpu.VMEM),
            pl.BlockSpec(memory_space=pltpu.VMEM),
        ],
        out_specs=pl.BlockSpec(memory_space=pltpu.VMEM),
    )(band, start_t)


def fir_kernel(left_ref, right_ref, prev_ref, cur_ref, next_ref, lo_ref, mid_ref, hi_ref, out_ref, *, first, last):
    block = (pl.program_id(0) + first) % (last + 1)
    before = jnp.where(block == 0, left_ref[...], prev_ref[...])
    after = jnp.where(block == last, right_ref[...], next_ref[...])
    out_ref[...] = (
        jnp.dot(before, lo_ref[...], preferred_element_type=jnp.float32)
        + jnp.dot(cur_ref[...], mid_ref[...], preferred_element_type=jnp.float32)
        + jnp.dot(after, hi_ref[...], preferred_element_type=jnp.float32)
    )


def fir(raw, left, right, band, start, length):
    chans, samples = raw.shape
    width = band.shape[1]
    edge = 128
    step = width // edge
    first = start // width
    blocks = samples // width
    lo, mid, hi = band[:edge], band[edge : edge + width], band[edge + width :]
    kernel = lambda *refs: fir_kernel(*refs, first=first, last=blocks - 1)
    full = lambda b: (0, 0)
    at = lambda b: (b + first) % blocks
    return pl.pallas_call(
        kernel,
        grid=(length // width,),
        out_shape=jax.ShapeDtypeStruct((chans, length), jnp.float32),
        in_specs=[
            pl.BlockSpec((chans, edge), full),
            pl.BlockSpec((chans, edge), full),
            pl.BlockSpec((chans, edge), lambda b: (0, jnp.maximum(at(b) * step - 1, 0))),
            pl.BlockSpec((chans, width), lambda b: (0, at(b))),
            pl.BlockSpec((chans, edge), lambda b: (0, jnp.minimum((at(b) + 1) * step, samples // edge - 1))),
            pl.BlockSpec((edge, width), full),
            pl.BlockSpec((width, width), full),
            pl.BlockSpec((edge, width), full),
        ],
        out_specs=pl.BlockSpec((chans, width), lambda b: (0, b)),
    )(left, right, raw, raw, raw, lo, mid, hi)


def clean_kernel(lower_ref, own_ref, upper_ref, basis_ref, middle_ref, *rest):
    out_ref = rest[-1]
    tiles = own_ref.shape[0] // STRIDE
    parts = [lower_ref[k * STRIDE : (k + 1) * STRIDE] for k in range(2)]
    parts += [own_ref[k * STRIDE : (k + 1) * STRIDE] for k in range(tiles)]
    parts.append(upper_ref[...])
    for number in range(tiles):
        coeffs = jnp.dot(basis_ref[number, :, 0:STRIDE], parts[number], preferred_element_type=jnp.float32)
        for k in range(1, WIN // STRIDE):
            coeffs = coeffs + jnp.dot(
                basis_ref[number, :, k * STRIDE : (k + 1) * STRIDE], parts[number + k],
                preferred_element_type=jnp.float32,
            )
        fitted = jnp.dot(
            middle_ref[number], coeffs.astype(jnp.bfloat16), preferred_element_type=jnp.float32
        )
        out_ref[number * STRIDE : (number + 1) * STRIDE] = (
            parts[number + 2].astype(jnp.float32) - fitted
        ).astype(out_ref.dtype)


def clean(lower, own, upper, rounded, total, start, into):
    chans, samples = own.shape
    width = math.gcd(math.gcd(samples, start) if start else samples, 512)
    first = start // width
    middle = jnp.swapaxes(rounded[:, :, 2 * STRIDE : 3 * STRIDE], 1, 2)
    return pl.pallas_call(
        clean_kernel,
        grid=(samples // width,),
        out_shape=jax.ShapeDtypeStruct((chans, total), own.dtype),
        in_specs=[
            pl.BlockSpec((lower.shape[0], width), lambda b: (0, b)),
            pl.BlockSpec((chans, width), lambda b: (0, b)),
            pl.BlockSpec((STRIDE, width), lambda b: (0, b)),
            pl.BlockSpec(rounded.shape, lambda b: (0, 0, 0)),
            pl.BlockSpec(middle.shape, lambda b: (0, 0, 0)),
        ] + ([] if into is None else [pl.BlockSpec(memory_space=pl.ANY)]),
        out_specs=pl.BlockSpec((chans, width), lambda b: (0, (b + first) % (total // width))),
        input_output_aliases={} if into is None else {5: 0},
    )(lower, own, upper, rounded, middle, *([] if into is None else [into]))


def ta_sum(value):
    count = lax.axis_size("ta")
    if count != 4:
        return lax.psum(value, "ta")
    core = lax.axis_index("ta") % 2
    rows = value.shape[0] // 2
    low, high = value[:rows], value[rows:]
    mine = jnp.where(core == 0, low, high)
    theirs = jnp.where(core == 0, high, low)
    partner = [(i, i ^ 1) for i in range(count)]
    across = [(i, i ^ 2) for i in range(count)]
    part = mine + lax.ppermute(theirs, "ta", partner)
    part = part + lax.ppermute(part, "ta", across)
    other = lax.ppermute(part, "ta", partner)
    return jnp.where(core == 0, jnp.concatenate([part, other]), jnp.concatenate([other, part]))


def per_device(raw, fir_taps, start_basis):
    chans = raw.shape[0]
    samples = raw.shape[1]
    half = (TAPS - 1) // 2
    count = lax.axis_size("ta")
    forward = [(i, i + 1) for i in range(count - 1)]
    backward = [(target, source) for source, target in forward]
    blank = jnp.zeros((chans, STRIDE - half), raw.dtype)
    left = jnp.concatenate([blank, lax.ppermute(raw[:, samples - half :], "ta", forward)], axis=1)
    right = jnp.concatenate([lax.ppermute(raw[:, :half], "ta", backward), blank], axis=1)
    width = math.gcd(samples, 512)
    band = jnp.pad(toeplitz_band(fir_taps, width), ((half, half), (0, 0)))
    chunks = 2 if samples % 1024 == 0 else 1
    piece = samples // chunks
    tiles = chans // STRIDE
    windows = tiles
    total_time = samples * lax.axis_size("ta")
    gaugeds, lowers, uppers = [], [], []
    own = cross_left = cross_right = None
    rimmed = jnp.concatenate(
        [shifted(raw[chans - GAUGE :], "ch", 1), raw, shifted(raw[:GAUGE], "ch", -1)], axis=0
    )
    source = raw
    for number in range(chunks):
        start = number * piece + width
        if number == chunks - 1:
            filtered = fir(source, left, right, band, start, piece)
            extended = with_halo(filtered, (("ch", 0),), GAUGE)
        else:
            extended = fir(rimmed, rimmed[:, :STRIDE], rimmed[:, :STRIDE], band, start, piece)
        gauged = (extended[2 * GAUGE :] - extended[: -2 * GAUGE]).astype(jnp.bfloat16)
        lower_part = shifted(gauged[chans - 2 * STRIDE :], "ch", 1)
        upper_part = shifted(gauged[:STRIDE], "ch", -1)
        local = gram(gauged, gauged)
        own = local if own is None else own + local
        gaugeds.append(gauged)
        lowers.append(lower_part)
        uppers.append(upper_part)
        source, left, right, gauged = lax.optimization_barrier((source, left, right, gauged))

    own = ta_sum(own)
    own_left = shifted(own[chans - 2 * STRIDE :, chans - 2 * STRIDE :], "ch", 1)
    own_right = shifted(own[:STRIDE, :STRIDE], "ch", -1)
    own, lowers, uppers = lax.optimization_barrier((own, lowers, uppers))

    for number in range(chunks):
        lower_part, gauged, upper_part = lowers[number], gaugeds[number], uppers[number]
        left = gram(lower_part, gauged)
        tail = jnp.concatenate([lower_part[STRIDE:], gauged], axis=0)
        right = gram(tail, upper_part)
        cross_left = left if cross_left is None else cross_left + left
        cross_right = right if cross_right is None else cross_right + right

    packed = ta_sum(jnp.concatenate([cross_left[:, :STRIDE], cross_left[:, STRIDE:], cross_right], axis=0))
    tiles_left = 2 * STRIDE
    cross_left = jnp.concatenate(
        [packed[:tiles_left], packed[tiles_left : 2 * tiles_left]], axis=1
    )
    cross_right = packed[2 * tiles_left :]

    zeros = jnp.zeros((STRIDE, STRIDE), jnp.float32)
    top = jnp.concatenate(
        [own_left, cross_left, jnp.concatenate([zeros, cross_right[:STRIDE]], axis=0)], axis=1
    )
    middle = jnp.concatenate(
        [cross_left.T, own, cross_right[STRIDE:]], axis=1
    )
    corner = jnp.concatenate([zeros, cross_right[:STRIDE].T], axis=1)
    bottom = jnp.concatenate([corner, cross_right[STRIDE:].T, own_right], axis=1)
    band = jnp.concatenate([top, middle, bottom], axis=0) / total_time

    rounded = subspace(band, start_basis.T, windows)
    cleaned = None
    for number in range(chunks):
        cleaned = clean(
            lowers[number], gaugeds[number], uppers[number], rounded, samples, number * piece + width, cleaned
        )
    return cleaned


def solution(mesh):
    return jax.shard_map(
        per_device,
        mesh=mesh,
        in_specs=(P("ch", "ta"), P(), P()),
        out_specs=P("ch", "ta"),
        check_vma=False,
    )
```

```python
import math

import jax
import jax.numpy as jnp
from jax import lax
from jax.experimental import pallas as pl
from jax.experimental.pallas import tpu as pltpu
from jax.sharding import PartitionSpec as P

TAPS = 129
GAUGE = 4
STRIDE = 128
RANK = 16
ITERS = 6
WIN = 512


def with_halo(block, sides, width):
    for axis, dim in sides:
        count = lax.axis_size(axis)
        forward = [(i, i + 1) for i in range(count - 1)]
        backward = [(target, source) for source, target in forward]
        low = lax.ppermute(
            lax.slice_in_dim(block, block.shape[dim] - width, None, axis=dim), axis, forward
        )
        high = lax.ppermute(lax.slice_in_dim(block, 0, width, axis=dim), axis, backward)
        block = jnp.concatenate([low, block, high], axis=dim)
    return block


def shifted(value, axis, steps):
    count = lax.axis_size(axis)
    first, last = (max(0, -steps), min(count, count - steps))
    return lax.ppermute(value, axis, [(source, source + steps) for source in range(first, last)])


def toeplitz_band(taps, width):
    count = taps.shape[0]
    line = jnp.concatenate([taps, jnp.zeros((width,), taps.dtype)])
    flat = jnp.tile(line, width)[: width * (count + width - 1)]
    return flat.reshape(width, count + width - 1).T


def gram(a, b):
    return lax.dot_general(a, b, (((1,), (1,)), ((), ())), preferred_element_type=jnp.float32)


def orthonormal_rows(image, rows, lanes):
    rank = image.shape[0]
    gram_mat = lax.dot_general(
        image, image, (((1,), (1,)), ((), ())), precision=lax.Precision.HIGHEST,
        preferred_element_type=jnp.float32,
    )
    result = image
    for j in range(rank):
        column = jnp.sum(jnp.where(lanes == j, gram_mat, 0.0), axis=1, keepdims=True)
        scale = 1.0 / jnp.sqrt(column[j : j + 1, :])
        factor = column * scale
        pivot_row = gram_mat[j : j + 1, :] * scale
        image_row = result[j : j + 1, :] * scale
        below = rows > j
        gram_mat = jnp.where(below, gram_mat - factor * pivot_row, gram_mat)
        result = jnp.where(below, result - factor * image_row, jnp.where(rows == j, image_row, result))
    return result


def subspace_kernel(band_ref, start_ref, out_ref):
    windows = out_ref.shape[0]
    rank, win = start_ref.shape
    rows = lax.broadcasted_iota(jnp.int32, (rank, 1), 0)
    lanes = lax.broadcasted_iota(jnp.int32, (rank, rank), 1)
    bases = [start_ref[...] for _ in range(windows)]
    for sweep in range(ITERS):
        for number in range(windows):
            lo = number * STRIDE
            scatter_mat = band_ref[lo : lo + win, lo : lo + win]
            image = jnp.dot(
                bases[number], scatter_mat, precision=lax.Precision.HIGHEST,
                preferred_element_type=jnp.float32,
            )
            bases[number] = orthonormal_rows(image, rows, lanes)
    for number in range(windows):
        out_ref[number] = bases[number].astype(out_ref.dtype)


def subspace(band, start_t, windows):
    return pl.pallas_call(
        subspace_kernel,
        out_shape=jax.ShapeDtypeStruct((windows,) + start_t.shape, jnp.bfloat16),
        in_specs=[
            pl.BlockSpec(memory_space=pltpu.VMEM),
            pl.BlockSpec(memory_space=pltpu.VMEM),
        ],
        out_specs=pl.BlockSpec(memory_space=pltpu.VMEM),
    )(band, start_t)


def fir_kernel(left_ref, right_ref, prev_ref, cur_ref, next_ref, lo_ref, mid_ref, hi_ref, out_ref, *, first, last):
    block = (pl.program_id(0) + first) % (last + 1)
    before = jnp.where(block == 0, left_ref[...], prev_ref[...])
    after = jnp.where(block == last, right_ref[...], next_ref[...])
    out_ref[...] = (
        jnp.dot(before, lo_ref[...], preferred_element_type=jnp.float32)
        + jnp.dot(cur_ref[...], mid_ref[...], preferred_element_type=jnp.float32)
        + jnp.dot(after, hi_ref[...], preferred_element_type=jnp.float32)
    )


def fir(raw, left, right, band, start, length):
    chans, samples = raw.shape
    width = band.shape[1]
    edge = 128
    step = width // edge
    first = start // width
    blocks = samples // width
    lo, mid, hi = band[:edge], band[edge : edge + width], band[edge + width :]
    kernel = lambda *refs: fir_kernel(*refs, first=first, last=blocks - 1)
    full = lambda b: (0, 0)
    at = lambda b: (b + first) % blocks
    return pl.pallas_call(
        kernel,
        grid=(length // width,),
        out_shape=jax.ShapeDtypeStruct((chans, length), jnp.float32),
        in_specs=[
            pl.BlockSpec((chans, edge), full),
            pl.BlockSpec((chans, edge), full),
            pl.BlockSpec((chans, edge), lambda b: (0, jnp.maximum(at(b) * step - 1, 0))),
            pl.BlockSpec((chans, width), lambda b: (0, at(b))),
            pl.BlockSpec((chans, edge), lambda b: (0, jnp.minimum((at(b) + 1) * step, samples // edge - 1))),
            pl.BlockSpec((edge, width), full),
            pl.BlockSpec((width, width), full),
            pl.BlockSpec((edge, width), full),
        ],
        out_specs=pl.BlockSpec((chans, width), lambda b: (0, b)),
    )(left, right, raw, raw, raw, lo, mid, hi)


def clean_kernel(lower_ref, own_ref, upper_ref, basis_ref, middle_ref, *rest):
    out_ref = rest[-1]
    tiles = own_ref.shape[0] // STRIDE
    rank = middle_ref.shape[2]
    span = WIN // STRIDE
    parts = [lower_ref[k * STRIDE : (k + 1) * STRIDE] for k in range(2)]
    parts += [own_ref[k * STRIDE : (k + 1) * STRIDE] for k in range(tiles)]
    parts.append(upper_ref[...])
    coeffs = [None] * tiles
    for k in range(len(parts)):
        users = [number for number in range(tiles) if number <= k < number + span]
        product = jnp.dot(basis_ref[k, : len(users) * rank], parts[k], preferred_element_type=jnp.float32)
        for slot, number in enumerate(users):
            piece = product[slot * rank : (slot + 1) * rank]
            coeffs[number] = piece if coeffs[number] is None else coeffs[number] + piece
    for number in range(tiles):
        fitted = jnp.dot(
            middle_ref[number], coeffs[number].astype(jnp.bfloat16), preferred_element_type=jnp.float32
        )
        out_ref[number * STRIDE : (number + 1) * STRIDE] = (
            parts[number + 2].astype(jnp.float32) - fitted
        ).astype(out_ref.dtype)


def stack_basis(rounded):
    windows, rank, win = rounded.shape
    span = win // STRIDE
    stacks = []
    for k in range(windows + span - 1):
        users = [number for number in range(windows) if number <= k < number + span]
        rows = [rounded[number, :, (k - number) * STRIDE : (k - number + 1) * STRIDE] for number in users]
        rows += [jnp.zeros((rank, STRIDE), rounded.dtype)] * (min(windows, span) - len(users))
        stacks.append(jnp.concatenate(rows, axis=0))
    return jnp.stack(stacks)


def clean(lower, own, upper, rounded, total, start, into):
    chans, samples = own.shape
    width = math.gcd(math.gcd(samples, start) if start else samples, 512)
    first = start // width
    middle = jnp.swapaxes(rounded[:, :, 2 * STRIDE : 3 * STRIDE], 1, 2)
    stacked = stack_basis(rounded)
    return pl.pallas_call(
        clean_kernel,
        grid=(samples // width,),
        out_shape=jax.ShapeDtypeStruct((chans, total), own.dtype),
        in_specs=[
            pl.BlockSpec((lower.shape[0], width), lambda b: (0, b)),
            pl.BlockSpec((chans, width), lambda b: (0, b)),
            pl.BlockSpec((STRIDE, width), lambda b: (0, b)),
            pl.BlockSpec(stacked.shape, lambda b: (0, 0, 0)),
            pl.BlockSpec(middle.shape, lambda b: (0, 0, 0)),
        ] + ([] if into is None else [pl.BlockSpec(memory_space=pl.ANY)]),
        out_specs=pl.BlockSpec((chans, width), lambda b: (0, (b + first) % (total // width))),
        input_output_aliases={} if into is None else {5: 0},
    )(lower, own, upper, stacked, middle, *([] if into is None else [into]))


def ta_sum(value):
    count = lax.axis_size("ta")
    if count != 4:
        return lax.psum(value, "ta")
    core = lax.axis_index("ta") % 2
    rows = value.shape[0] // 2
    low, high = value[:rows], value[rows:]
    mine = jnp.where(core == 0, low, high)
    theirs = jnp.where(core == 0, high, low)
    partner = [(i, i ^ 1) for i in range(count)]
    across = [(i, i ^ 2) for i in range(count)]
    part = mine + lax.ppermute(theirs, "ta", partner)
    part = part + lax.ppermute(part, "ta", across)
    other = lax.ppermute(part, "ta", partner)
    return jnp.where(core == 0, jnp.concatenate([part, other]), jnp.concatenate([other, part]))


def per_device(raw, fir_taps, start_basis):
    chans = raw.shape[0]
    samples = raw.shape[1]
    half = (TAPS - 1) // 2
    count = lax.axis_size("ta")
    forward = [(i, i + 1) for i in range(count - 1)]
    backward = [(target, source) for source, target in forward]
    blank = jnp.zeros((chans, STRIDE - half), raw.dtype)
    left = jnp.concatenate([blank, lax.ppermute(raw[:, samples - half :], "ta", forward)], axis=1)
    right = jnp.concatenate([lax.ppermute(raw[:, :half], "ta", backward), blank], axis=1)
    width = math.gcd(samples, 512)
    band = jnp.pad(toeplitz_band(fir_taps, width), ((half, half), (0, 0)))
    chunks = 2 if samples % 1024 == 0 else 1
    piece = samples // chunks
    tiles = chans // STRIDE
    windows = tiles
    total_time = samples * lax.axis_size("ta")
    gaugeds, lowers, uppers = [], [], []
    own = cross_left = cross_right = None
    rimmed = jnp.concatenate(
        [shifted(raw[chans - GAUGE :], "ch", 1), raw, shifted(raw[:GAUGE], "ch", -1)], axis=0
    )
    filters = []
    for number in range(chunks):
        start = number * piece + width
        if number == chunks - 1:
            filters.append(fir(raw, left, right, band, start, piece))
        else:
            filters.append(fir(rimmed, rimmed[:, :STRIDE], rimmed[:, :STRIDE], band, start, piece))
    filters = lax.optimization_barrier(filters)
    for number in range(chunks):
        if number == chunks - 1:
            extended = with_halo(filters[number], (("ch", 0),), GAUGE)
        else:
            extended = filters[number]
        gauged = (extended[2 * GAUGE :] - extended[: -2 * GAUGE]).astype(jnp.bfloat16)
        lower_part = shifted(gauged[chans - 2 * STRIDE :], "ch", 1)
        upper_part = shifted(gauged[:STRIDE], "ch", -1)
        local = gram(gauged, gauged)
        own = local if own is None else own + local
        gaugeds.append(gauged)
        lowers.append(lower_part)
        uppers.append(upper_part)

    own = ta_sum(own)
    own_left = shifted(own[chans - 2 * STRIDE :, chans - 2 * STRIDE :], "ch", 1)
    own_right = shifted(own[:STRIDE, :STRIDE], "ch", -1)
    own, lowers, uppers = lax.optimization_barrier((own, lowers, uppers))

    for number in range(chunks):
        lower_part, gauged, upper_part = lowers[number], gaugeds[number], uppers[number]
        left = gram(lower_part, gauged)
        tail = jnp.concatenate([lower_part[STRIDE:], gauged], axis=0)
        right = gram(tail, upper_part)
        cross_left = left if cross_left is None else cross_left + left
        cross_right = right if cross_right is None else cross_right + right

    packed = ta_sum(jnp.concatenate([cross_left[:, :STRIDE], cross_left[:, STRIDE:], cross_right], axis=0))
    tiles_left = 2 * STRIDE
    cross_left = jnp.concatenate(
        [packed[:tiles_left], packed[tiles_left : 2 * tiles_left]], axis=1
    )
    cross_right = packed[2 * tiles_left :]

    zeros = jnp.zeros((STRIDE, STRIDE), jnp.float32)
    top = jnp.concatenate(
        [own_left, cross_left, jnp.concatenate([zeros, cross_right[:STRIDE]], axis=0)], axis=1
    )
    middle = jnp.concatenate(
        [cross_left.T, own, cross_right[STRIDE:]], axis=1
    )
    corner = jnp.concatenate([zeros, cross_right[:STRIDE].T], axis=1)
    bottom = jnp.concatenate([corner, cross_right[STRIDE:].T, own_right], axis=1)
    band = jnp.concatenate([top, middle, bottom], axis=0) / total_time

    rounded = subspace(band, start_basis.T, windows)
    cleaned = None
    for number in range(chunks):
        cleaned = clean(
            lowers[number], gaugeds[number], uppers[number], rounded, samples, number * piece + width, cleaned
        )
    return cleaned


def solution(mesh):
    return jax.shard_map(
        per_device,
        mesh=mesh,
        in_specs=(P("ch", "ta"), P(), P()),
        out_specs=P("ch", "ta"),
        check_vma=False,
    )
```
